256 devices in a mesh: rows: 32 (over x, z), cols: 8 (over y, core).
Axes of the slice: x: 4, y: 4, z: 8, core: 2. Of those that a mesh axis runs over, the one named last changes fastest.
Arguments:
- graph_tiles: bfloat16 [512, 17, 128, 128], P('rows'), as said below
- tile_column: int32 [512, 17], P('rows'), may hold values from 0 to 511, as said below
- tile_count: int32 [512], P('rows'), may hold values from 1 to 17, as said below
- class_label: int32 [65536], P('rows'), may hold values from 0 to 999
- confidence: float32 [65536], P('rows'), may hold values from 0.2 to 1
- class_weight: float32 [1000], P('cols'), may hold values from 0.25 to 4
Outputs:
- scores: float32 [65536, 1000], P('rows', 'cols')
- residual: float32 [65536, 1000], P('rows', 'cols')
The draws below stay inside these ranges and needn't reach their ends.
Inputs may be any that keep to these rules, and one draw needn't show every extreme that they name: `tile_column`: Block-row i's live tiles lie in distinct block-columns (i + d) mod 512 with |d| <= 8; block-row i has a live tile in block-column j exactly when block-row j has one in block-column i. `tile_count`: slots at and beyond a block-row's count are unused. `graph_tiles`: the matrix S assembled from the live tiles is symmetric: the tile of block-row i in block-column j is the transpose of the tile of block-row j in block-column i. Entries of a live tile of block-row i in block-column j lie between 0 and 1 / (128 * sqrt(tile_count[i] * tile_count[j])).
All inputs are finite; a program needn't handle non-finite values.
Results may differ from the reference program's by a relative error of at most 0.003.
Values may be sent and summed in bfloat16 or wider, within the bound.
No kernel may reach another device: no remote copies, remote signals or barrier semaphores. Data moves between devices by JAX's collectives and lax.ppermute only.
A program may use at most 128 MiB of HBM per device.

```python
import math
import jax
import jax.numpy as jnp
import numpy as np
from jax import lax

C = 1000
B = 128
ITERS = 3
BR_DEV = 16
HALF = 8
KMAX = 17
NB = 512
NROWS = 65536


def graph_pattern(key):
    keys = jax.random.split(jax.random.fold_in(key, 101), 3)
    row_ids = jnp.arange(NB, dtype=jnp.int32)
    distance = jnp.arange(1, HALF + 1, dtype=jnp.int32)
    level = jax.random.randint(keys[0], (NB // BR_DEV,), 1, 9)
    level_rows = jnp.repeat(level, BR_DEV)
    coins = jax.random.randint(keys[1], (NB, HALF), 0, 8)
    pair_bits = coins < level_rows[:, None]
    first_row = jax.random.randint(keys[2], (), 0, NB)
    second_row = jnp.mod(first_row + NB // 2, NB)
    partner = jnp.mod(row_ids[:, None] + distance[None, :], NB)
    touch_first = (row_ids[:, None] == first_row) | (partner == first_row)
    touch_second = (row_ids[:, None] == second_row) | (partner == second_row)
    pair_bits = jnp.where(touch_first, True, pair_bits)
    pair_bits = jnp.where(touch_second, False, pair_bits)
    plus_live = pair_bits
    behind = jnp.mod(row_ids[:, None] - distance[None, :], NB)
    minus_live = pair_bits[behind, jnp.arange(HALF, dtype=jnp.int32)[None, :]]
    side_live = jnp.stack([plus_live, minus_live], axis=2).reshape(NB, 2 * HALF)
    live = jnp.concatenate([jnp.ones((NB, 1), dtype=bool), side_live], axis=1)
    offset_table = jnp.stack([distance, -distance], axis=1).reshape(2 * HALF)
    offset_table = jnp.concatenate([jnp.zeros((1,), jnp.int32), offset_table])
    counts = jnp.sum(live.astype(jnp.int32), axis=1).astype(jnp.int32)
    order = jnp.argsort(1 - live.astype(jnp.int32), axis=1, stable=True)
    live_sorted = jnp.take_along_axis(live, order, axis=1)
    offset_sorted = offset_table[order]
    columns = jnp.where(live_sorted, jnp.mod(row_ids[:, None] + offset_sorted, NB), row_ids[:, None])
    return (order, live_sorted, columns.astype(jnp.int32), counts)


def draw_graph_tiles(key, part):
    order, live_sorted, columns, counts = graph_pattern(key)
    raw = jax.random.uniform(jax.random.fold_in(key, 202), (NB, HALF + 1, B, B), jnp.float32)
    base = 1.0 - 0.5 * raw
    row_ids = jnp.arange(NB, dtype=jnp.int32)
    diagonal_tile = 0.5 * (base[:, 0] + jnp.swapaxes(base[:, 0], 1, 2))
    pieces = [diagonal_tile]
    for dist in range(1, HALF + 1):
        pieces.append(base[:, dist])
        behind = jnp.mod(row_ids - dist, NB)
        pieces.append(jnp.swapaxes(base[behind, dist], 1, 2))
    candidates = jnp.stack(pieces, axis=1)
    sorted_tiles = jnp.take_along_axis(candidates, order[:, :, None, None], axis=1)
    own_count = counts.astype(jnp.float32)[:, None]
    other_count = counts[columns].astype(jnp.float32)
    scale = 1.0 / (B * jnp.sqrt(own_count * other_count))
    scale = jnp.where(live_sorted, scale, 0.0)
    return (sorted_tiles * scale[:, :, None, None]).astype(jnp.bfloat16)


def draw_tile_column(key, part):
    order, live_sorted, columns, counts = graph_pattern(key)
    return columns


def draw_tile_count(key, part):
    order, live_sorted, columns, counts = graph_pattern(key)
    return counts


def with_ends(drawn, key, low, largest):
    shape = drawn.shape
    spot = [jax.random.randint(jax.random.fold_in(key, axis), (), 0, shape[axis]) for axis in range(len(shape))]
    drawn = drawn.at[tuple(spot)].set(low)
    longest = shape.index(max(shape))
    spot[longest] = (spot[longest] + 1) % shape[longest]
    return drawn.at[tuple(spot)].set(largest)


def shard_levels(rng, shape, cuts, low, high):
    gain, own = 1.0, jax.random.fold_in(rng, 6)
    for axis_at, shards_of in cuts:
        steps = jnp.exp(jax.random.uniform(jax.random.fold_in(own, axis_at), (shards_of,), jnp.float32, low / len(cuts), high / len(cuts)))
        gain = gain * jnp.repeat(steps, shape[axis_at] // shards_of).reshape([-1 if axis == axis_at else 1 for axis in range(len(shape))])
    return gain


def cumulative_ranks(count, slope):
    loads = [(1 << 20) // math.isqrt(rank ** slope) + 1 for rank in range(1, count + 1)]
    spread = 1 + sum(loads) // (1 << 30)
    return np.cumsum(np.array([max(1, weight // spread) for weight in loads]))


def skewed_ids(key, shape, number_of, lean):
    grid = cumulative_ranks(number_of, lean)
    lot = jax.random.randint(jax.random.fold_in(key, 1), shape, 0, int(grid[number_of - 1]))
    rank = jnp.searchsorted(jnp.asarray(grid, jnp.int32), lot, side="right")
    return jax.random.permutation(jax.random.fold_in(key, 2), number_of)[rank].astype(jnp.int32)


def setup_inputs(seed: int = 0) -> dict:
    key_list = jax.random.split(jax.random.key(seed), 7)
    return {
        "graph_tiles": draw_graph_tiles(jax.random.fold_in(key_list[6], 71), 0),
        "tile_column": draw_tile_column(jax.random.fold_in(key_list[6], 71), 0),
        "tile_count": draw_tile_count(jax.random.fold_in(key_list[6], 71), 0),
        "class_label": with_ends(skewed_ids(key_list[3], (NROWS,), C, 2), jax.random.fold_in(key_list[3], 3), 0, C - 1).astype(jnp.int32),
        "confidence": jnp.clip(jnp.exp(math.log(1.0) - 1.609438 * jax.random.uniform(key_list[4], (NROWS,), jnp.float32) ** shard_levels(key_list[4], (NROWS,), ((0, 32),), -0.2, 0.2)), 0.2, 1.0),
        "class_weight": jnp.clip(jnp.exp(math.log(4.0) - 2.7725887 * jax.random.uniform(key_list[5], (C,), jnp.float32) ** shard_levels(key_list[5], (C,), ((0, 8),), -0.2, 0.2)), 0.25, 4.0),
    }


damping = 0.99
smoothing = 0.1

def apply_operator(direction, graph_tiles, tile_column, live_slot):
    rounded = lax.optimization_barrier(direction.astype(jnp.bfloat16))
    blocks = rounded.reshape(NB, B, C)
    product_sum = jnp.zeros((NB, B, C), jnp.float32)
    for slot in range(KMAX):
        picked = blocks[tile_column[:, slot]].astype(jnp.float32)
        picked = jnp.where(live_slot[:, slot][:, None, None], picked, jnp.float32(0.0))
        tile_slot = graph_tiles[:, slot].astype(jnp.float32)
        product_sum = product_sum + jnp.einsum('rij,rjc->ric', tile_slot, picked)
    return direction - damping * product_sum.reshape(NROWS, C)

def reference(graph_tiles, tile_column, tile_count, class_label, confidence, class_weight):
    live_slot = jnp.arange(KMAX, dtype=jnp.int32)[None, :] < tile_count[:, None]
    onehot = (class_label[:, None] == jnp.arange(C, dtype=jnp.int32)[None, :]).astype(jnp.float32)
    prior_labels = confidence[:, None] * class_weight[None, :] * ((1.0 - smoothing) * onehot + smoothing / C)
    solution = jnp.zeros_like(prior_labels)
    residual = prior_labels
    direction = prior_labels
    norm_now = lax.optimization_barrier(jnp.sum(residual * residual, axis=0))
    for step in range(ITERS):
        applied = apply_operator(direction, graph_tiles, tile_column, live_slot)
        step_size = norm_now / lax.optimization_barrier(jnp.sum(direction * applied, axis=0))
        solution = solution + step_size[None, :] * direction
        residual = residual - step_size[None, :] * applied
        norm_next = lax.optimization_barrier(jnp.sum(residual * residual, axis=0))
        direction = residual + (norm_next / norm_now)[None, :] * direction
        norm_now = norm_next
    length = jnp.sqrt(lax.optimization_barrier(jnp.sum(solution * solution, axis=1, keepdims=True)) + 1e-06)
    return (solution / length, residual)
```

```python
import jax
import jax.numpy as jnp
from jax import lax
from jax.sharding import Mesh, PartitionSpec as P

ITERS = 3
ROWS = ("rx", "rz")
COLS = ("cy", "cc")


damping = 0.99
smoothing = 0.1


def padded(cells, sides, width):
    for axis, dim in sides:
        count = lax.axis_size(axis)
        head = lax.slice_in_dim(cells, 0, width, axis=dim)
        tail = lax.slice_in_dim(cells, cells.shape[dim] - width, cells.shape[dim], axis=dim)
        cells = jnp.concatenate(
            [
                lax.ppermute(tail, axis, [(i, (i + 1) % count) for i in range(count)]),
                cells,
                lax.ppermute(head, axis, [((i + 1) % count, i) for i in range(count)]),
            ],
            axis=dim,
        )
    return cells


def rows_sum(v):
    return lax.psum(lax.psum(v, "rz"), "rx")


def cols_sum(v):
    return lax.psum(lax.psum(v, "cc"), "cy")


def body(graph_tiles, tile_column, tile_count, class_label, confidence, class_weight):
    block_rows = graph_tiles.shape[0]
    slot_count = graph_tiles.shape[1]
    block_size = graph_tiles.shape[2]
    class_dev = class_weight.shape[0]
    half_span = block_rows // 2
    total_blocks = block_rows * lax.axis_size(ROWS)
    first_row = lax.axis_index(ROWS) * block_rows - half_span
    local_col = jnp.mod(tile_column - first_row, total_blocks)
    live_slot = jnp.arange(slot_count, dtype=jnp.int32)[None, :] < tile_count[:, None]
    class_ids = lax.axis_index(COLS) * class_dev + jnp.arange(class_dev, dtype=jnp.int32)
    onehot = (class_label[:, None] == class_ids[None, :]).astype(jnp.float32)
    prior_labels = (
        confidence[:, None]
        * class_weight[None, :]
        * ((1.0 - smoothing) * onehot + smoothing / (class_dev * lax.axis_size(COLS)))
    )
    zero_half = jnp.zeros((), jnp.bfloat16)

    def squares(residual):
        return rows_sum(jnp.sum(residual * residual, axis=0))

    solution = jnp.zeros_like(prior_labels)
    residual = prior_labels
    direction = prior_labels
    norm_now = squares(residual)
    for step in range(ITERS):
        extended = padded(direction.astype(jnp.bfloat16), ((ROWS, 0),), half_span * block_size)
        blocks = extended.reshape(block_rows + 2 * half_span, block_size, class_dev)
        picked = blocks[local_col]
        picked = jnp.where(live_slot[:, :, None, None], picked, zero_half)
        product_sum = jnp.einsum(
            "rkij,rkjc->ric", graph_tiles, picked, preferred_element_type=jnp.float32
        )
        applied = direction - damping * product_sum.reshape(block_rows * block_size, class_dev)
        curve_sum = rows_sum(jnp.sum(direction * applied, axis=0))
        step_size = norm_now / curve_sum
        solution = solution + step_size[None, :] * direction
        residual = residual - step_size[None, :] * applied
        norm_next = squares(residual)
        direction = residual + (norm_next / norm_now)[None, :] * direction
        norm_now = norm_next
    row_squares = cols_sum(jnp.sum(solution * solution, axis=1))
    length = jnp.sqrt(row_squares + 1e-06)
    return (solution / length[:, None], residual)


def factor(devices, pick):
    total = devices.shape[0]
    inner = len({pick(d) for d in devices})
    if inner < 1 or total % inner:
        return (1, total)
    return (total // inner, inner)


def solution(mesh):
    grid = mesh.devices
    row_shape = factor(grid[:, 0], lambda d: d.coords[2])
    col_shape = factor(grid[0, :], lambda d: d.core_on_chip)
    split = Mesh(grid.reshape(row_shape + col_shape), ROWS + COLS)
    placed = (
        P(ROWS, None, None, None),
        P(ROWS, None),
        P(ROWS),
        P(ROWS),
        P(ROWS),
        P(COLS),
    )
    return jax.shard_map(
        body,
        mesh=split,
        in_specs=placed,
        out_specs=(P(ROWS, COLS), P(ROWS, COLS)),
        check_vma=False,
    )
```

```python
import jax
import jax.numpy as jnp
from jax import lax
from jax.experimental import pallas as pl
from jax.experimental.pallas import tpu as pltpu
from jax.sharding import Mesh, PartitionSpec as P

ITERS = 3
ROWS = ("rx", "rz")
COLS = ("cy", "cc")


damping = 0.99
smoothing = 0.1


def padded(cells, sides, width):
    for axis, dim in sides:
        count = lax.axis_size(axis)
        head = lax.slice_in_dim(cells, 0, width, axis=dim)
        tail = lax.slice_in_dim(cells, cells.shape[dim] - width, cells.shape[dim], axis=dim)
        cells = jnp.concatenate(
            [
                lax.ppermute(tail, axis, [(i, (i + 1) % count) for i in range(count)]),
                cells,
                lax.ppermute(head, axis, [((i + 1) % count, i) for i in range(count)]),
            ],
            axis=dim,
        )
    return cells


def rows_sum(v):
    return lax.psum(lax.psum(v, "rz"), "rx")


def cols_sum(v):
    return lax.psum(lax.psum(v, "cc"), "cy")


def tile_kernel(col_ref, count_ref, tile_ref, vec_ref, out_ref):
    row = pl.program_id(0)
    slots = tile_ref.shape[1]
    size = tile_ref.shape[2]
    live = count_ref[row]
    out_ref[...] = jnp.zeros(out_ref.shape, out_ref.dtype)
    for slot in range(slots):

        @pl.when(slot < live)
        def _():
            start = pl.multiple_of(col_ref[row * slots + slot] * size, size)
            block = vec_ref[pl.ds(start, size), :]
            out_ref[...] += jnp.dot(
                tile_ref[0, slot], block, preferred_element_type=jnp.float32
            )


def block_product(graph_tiles, local_col, tile_count, extended):
    block_rows, slot_count, size, _ = graph_tiles.shape
    width = extended.shape[1]
    grid_spec = pltpu.PrefetchScalarGridSpec(
        num_scalar_prefetch=2,
        grid=(block_rows,),
        in_specs=[
            pl.BlockSpec((1, slot_count, size, size), lambda r, c, n: (r, 0, 0, 0)),
            pl.BlockSpec(extended.shape, lambda r, c, n: (0, 0)),
        ],
        out_specs=pl.BlockSpec((size, width), lambda r, c, n: (r, 0)),
    )
    cost = pl.CostEstimate(
        flops=2 * block_rows * slot_count * size * size * width,
        bytes_accessed=graph_tiles.size * 2 + extended.size * 2 + block_rows * size * width * 4,
        transcendentals=0,
    )
    return pl.pallas_call(
        tile_kernel,
        grid_spec=grid_spec,
        out_shape=jax.ShapeDtypeStruct((block_rows * size, width), jnp.float32),
        cost_estimate=cost,
    )(local_col.reshape(-1), tile_count, graph_tiles, extended)


def body(graph_tiles, tile_column, tile_count, class_label, confidence, class_weight):
    block_rows = graph_tiles.shape[0]
    slot_count = graph_tiles.shape[1]
    block_size = graph_tiles.shape[2]
    class_dev = class_weight.shape[0]
    half_span = block_rows // 2
    total_blocks = block_rows * lax.axis_size(ROWS)
    first_row = lax.axis_index(ROWS) * block_rows - half_span
    live_slot = jnp.arange(slot_count, dtype=jnp.int32)[None, :] < tile_count[:, None]
    local_col = jnp.where(live_slot, jnp.mod(tile_column - first_row, total_blocks), 0)
    class_ids = lax.axis_index(COLS) * class_dev + jnp.arange(class_dev, dtype=jnp.int32)
    onehot = (class_label[:, None] == class_ids[None, :]).astype(jnp.float32)
    prior_labels = (
        confidence[:, None]
        * class_weight[None, :]
        * ((1.0 - smoothing) * onehot + smoothing / (class_dev * lax.axis_size(COLS)))
    )

    def squares(residual):
        return rows_sum(jnp.sum(residual * residual, axis=0))

    solution = jnp.zeros_like(prior_labels)
    residual = prior_labels
    direction = prior_labels
    norm_now = squares(residual)
    for step in range(ITERS):
        extended = padded(direction.astype(jnp.bfloat16), ((ROWS, 0),), half_span * block_size)
        product_sum = block_product(graph_tiles, local_col, tile_count, extended)
        applied = direction - damping * product_sum
        curve_sum = rows_sum(jnp.sum(direction * applied, axis=0))
        step_size = norm_now / curve_sum
        solution = solution + step_size[None, :] * direction
        residual = residual - step_size[None, :] * applied
        norm_next = squares(residual)
        direction = residual + (norm_next / norm_now)[None, :] * direction
        norm_now = norm_next
    row_squares = cols_sum(jnp.sum(solution * solution, axis=1))
    length = jnp.sqrt(row_squares + 1e-06)
    return (solution / length[:, None], residual)


def factor(devices, pick):
    total = devices.shape[0]
    inner = len({pick(d) for d in devices})
    if inner < 1 or total % inner:
        return (1, total)
    return (total // inner, inner)


def solution(mesh):
    grid = mesh.devices
    row_shape = factor(grid[:, 0], lambda d: d.coords[2])
    col_shape = factor(grid[0, :], lambda d: d.core_on_chip)
    split = Mesh(grid.reshape(row_shape + col_shape), ROWS + COLS)
    placed = (
        P(ROWS, None, None, None),
        P(ROWS, None),
        P(ROWS),
        P(ROWS),
        P(ROWS),
        P(COLS),
    )
    return jax.shard_map(
        body,
        mesh=split,
        in_specs=placed,
        out_specs=(P(ROWS, COLS), P(ROWS, COLS)),
        check_vma=False,
    )
```

```python
import jax
import jax.numpy as jnp
from jax import lax
from jax.experimental import pallas as pl
from jax.experimental.pallas import tpu as pltpu
from jax.sharding import Mesh, PartitionSpec as P

ITERS = 3
ROWS = ("rx", "rz")
COLS = ("cy", "cc")


damping = 0.99
smoothing = 0.1


def padded(cells, sides, width):
    for axis, dim in sides:
        count = lax.axis_size(axis)
        head = lax.slice_in_dim(cells, 0, width, axis=dim)
        tail = lax.slice_in_dim(cells, cells.shape[dim] - width, cells.shape[dim], axis=dim)
        cells = jnp.concatenate(
            [
                lax.ppermute(tail, axis, [(i, (i + 1) % count) for i in range(count)]),
                cells,
                lax.ppermute(head, axis, [((i + 1) % count, i) for i in range(count)]),
            ],
            axis=dim,
        )
    return cells


def rows_sum(v):
    return lax.psum(lax.psum(v, "rz"), "rx")


def cols_sum(v):
    return lax.psum(lax.psum(v, "cc"), "cy")


def tile_kernel(col_ref, count_ref, tile_ref, vec_ref, out_ref):
    row = pl.program_id(0)
    slots = tile_ref.shape[1]
    size = tile_ref.shape[2]
    live = count_ref[row]
    lhs = jnp.concatenate([tile_ref[0, slot] for slot in range(slots)], axis=1)
    pieces = []
    for slot in range(slots):
        start = pl.multiple_of(col_ref[row * slots + slot] * size, size)
        block = vec_ref[pl.ds(start, size), :]
        pieces.append(jnp.where(slot < live, block, jnp.zeros_like(block)))
    rhs = jnp.concatenate(pieces, axis=0)
    out_ref[...] = jnp.dot(lhs, rhs, preferred_element_type=jnp.float32)


def block_product(graph_tiles, local_col, tile_count, extended):
    block_rows, slot_count, size, _ = graph_tiles.shape
    width = extended.shape[1]
    grid_spec = pltpu.PrefetchScalarGridSpec(
        num_scalar_prefetch=2,
        grid=(block_rows,),
        in_specs=[
            pl.BlockSpec((1, slot_count, size, size), lambda r, c, n: (r, 0, 0, 0)),
            pl.BlockSpec(extended.shape, lambda r, c, n: (0, 0)),
        ],
        out_specs=pl.BlockSpec((size, width), lambda r, c, n: (r, 0)),
    )
    cost = pl.CostEstimate(
        flops=2 * block_rows * slot_count * size * size * width,
        bytes_accessed=graph_tiles.size * 2 + extended.size * 2 + block_rows * size * width * 4,
        transcendentals=0,
    )
    return pl.pallas_call(
        tile_kernel,
        grid_spec=grid_spec,
        out_shape=jax.ShapeDtypeStruct((block_rows * size, width), jnp.float32),
        cost_estimate=cost,
    )(local_col.reshape(-1), tile_count, graph_tiles, extended)


def body(graph_tiles, tile_column, tile_count, class_label, confidence, class_weight):
    block_rows = graph_tiles.shape[0]
    slot_count = graph_tiles.shape[1]
    block_size = graph_tiles.shape[2]
    class_dev = class_weight.shape[0]
    half_span = block_rows // 2
    total_blocks = block_rows * lax.axis_size(ROWS)
    first_row = lax.axis_index(ROWS) * block_rows - half_span
    live_slot = jnp.arange(slot_count, dtype=jnp.int32)[None, :] < tile_count[:, None]
    local_col = jnp.where(live_slot, jnp.mod(tile_column - first_row, total_blocks), 0)
    class_ids = lax.axis_index(COLS) * class_dev + jnp.arange(class_dev, dtype=jnp.int32)
    onehot = (class_label[:, None] == class_ids[None, :]).astype(jnp.float32)
    prior_labels = (
        confidence[:, None]
        * class_weight[None, :]
        * ((1.0 - smoothing) * onehot + smoothing / (class_dev * lax.axis_size(COLS)))
    )

    def squares(residual):
        return rows_sum(jnp.sum(residual * residual, axis=0))

    solution = jnp.zeros_like(prior_labels)
    residual = prior_labels
    direction = prior_labels
    norm_now = squares(residual)
    for step in range(ITERS):
        extended = padded(direction.astype(jnp.bfloat16), ((ROWS, 0),), half_span * block_size)
        lanes = -class_dev % 128
        extended = jnp.pad(extended, ((0, 0), (0, lanes)))
        product_sum = block_product(graph_tiles, local_col, tile_count, extended)
        applied = direction - damping * product_sum[:, :class_dev]
        curve_sum = rows_sum(jnp.sum(direction * applied, axis=0))
        step_size = norm_now / curve_sum
        solution = solution + step_size[None, :] * direction
        residual = residual - step_size[None, :] * applied
        norm_next = squares(residual)
        direction = residual + (norm_next / norm_now)[None, :] * direction
        norm_now = norm_next
    row_squares = cols_sum(jnp.sum(solution * solution, axis=1))
    length = jnp.sqrt(row_squares + 1e-06)
    return (solution / length[:, None], residual)


def factor(devices, pick):
    total = devices.shape[0]
    inner = len({pick(d) for d in devices})
    if inner < 1 or total % inner:
        return (1, total)
    return (total // inner, inner)


def solution(mesh):
    grid = mesh.devices
    row_shape = factor(grid[:, 0], lambda d: d.coords[2])
    col_shape = factor(grid[0, :], lambda d: d.core_on_chip)
    split = Mesh(grid.reshape(row_shape + col_shape), ROWS + COLS)
    placed = (
        P(ROWS, None, None, None),
        P(ROWS, None),
        P(ROWS),
        P(ROWS),
        P(ROWS),
        P(COLS),
    )
    return jax.shard_map(
        body,
        mesh=split,
        in_specs=placed,
        out_specs=(P(ROWS, COLS), P(ROWS, COLS)),
        check_vma=False,
    )
```

```python
import jax
import jax.numpy as jnp
from jax import lax
from jax.experimental import pallas as pl
from jax.experimental.pallas import tpu as pltpu
from jax.sharding import Mesh, PartitionSpec as P

ITERS = 3
ROWS = ("rx", "rz")
COLS = ("cy", "cc")


damping = 0.99
smoothing = 0.1


def padded(cells, sides, width):
    for axis, dim in sides:
        count = lax.axis_size(axis)
        head = lax.slice_in_dim(cells, 0, width, axis=dim)
        tail = lax.slice_in_dim(cells, cells.shape[dim] - width, cells.shape[dim], axis=dim)
        cells = jnp.concatenate(
            [
                lax.ppermute(tail, axis, [(i, (i + 1) % count) for i in range(count)]),
                cells,
                lax.ppermute(head, axis, [((i + 1) % count, i) for i in range(count)]),
            ],
            axis=dim,
        )
    return cells


def rows_sum(v):
    count = lax.axis_size(ROWS)
    spread = jnp.broadcast_to(v[None], (count,) + v.shape)
    gathered = lax.all_to_all(spread, ROWS, 0, 0, tiled=True)
    return jnp.sum(gathered, axis=0)


def cols_sum(v):
    return lax.psum(lax.psum(v, "cc"), "cy")


def tile_kernel(col_ref, count_ref, tile_ref, vec_ref, out_ref):
    row = pl.program_id(0)
    slots = tile_ref.shape[1]
    size = tile_ref.shape[2]
    live = count_ref[row]
    lhs = jnp.concatenate([tile_ref[0, slot] for slot in range(slots)], axis=1)
    pieces = []
    for slot in range(slots):
        start = pl.multiple_of(col_ref[row * slots + slot] * size, size)
        block = vec_ref[pl.ds(start, size), :]
        pieces.append(jnp.where(slot < live, block, jnp.zeros_like(block)))
    rhs = jnp.concatenate(pieces, axis=0)
    out_ref[...] = jnp.dot(lhs, rhs, preferred_element_type=jnp.float32)


def block_product(graph_tiles, local_col, tile_count, extended):
    block_rows, slot_count, size, _ = graph_tiles.shape
    width = extended.shape[1]
    grid_spec = pltpu.PrefetchScalarGridSpec(
        num_scalar_prefetch=2,
        grid=(block_rows,),
        in_specs=[
            pl.BlockSpec((1, slot_count, size, size), lambda r, c, n: (r, 0, 0, 0)),
            pl.BlockSpec(extended.shape, lambda r, c, n: (0, 0)),
        ],
        out_specs=pl.BlockSpec((size, width), lambda r, c, n: (r, 0)),
    )
    cost = pl.CostEstimate(
        flops=2 * block_rows * slot_count * size * size * width,
        bytes_accessed=graph_tiles.size * 2 + extended.size * 2 + block_rows * size * width * 4,
        transcendentals=0,
    )
    return pl.pallas_call(
        tile_kernel,
        grid_spec=grid_spec,
        out_shape=jax.ShapeDtypeStruct((block_rows * size, width), jnp.float32),
        cost_estimate=cost,
    )(local_col.reshape(-1), tile_count, graph_tiles, extended)


def body(graph_tiles, tile_column, tile_count, class_label, confidence, class_weight):
    block_rows = graph_tiles.shape[0]
    slot_count = graph_tiles.shape[1]
    block_size = graph_tiles.shape[2]
    class_dev = class_weight.shape[0]
    half_span = block_rows // 2
    total_blocks = block_rows * lax.axis_size(ROWS)
    first_row = lax.axis_index(ROWS) * block_rows - half_span
    live_slot = jnp.arange(slot_count, dtype=jnp.int32)[None, :] < tile_count[:, None]
    local_col = jnp.where(live_slot, jnp.mod(tile_column - first_row, total_blocks), 0)
    class_ids = lax.axis_index(COLS) * class_dev + jnp.arange(class_dev, dtype=jnp.int32)
    onehot = (class_label[:, None] == class_ids[None, :]).astype(jnp.float32)
    prior_labels = (
        confidence[:, None]
        * class_weight[None, :]
        * ((1.0 - smoothing) * onehot + smoothing / (class_dev * lax.axis_size(COLS)))
    )

    def squares(residual):
        return rows_sum(jnp.sum(residual * residual, axis=0))

    solution = jnp.zeros_like(prior_labels)
    residual = prior_labels
    direction = prior_labels
    norm_now = None
    for step in range(ITERS):
        extended = padded(direction.astype(jnp.bfloat16), ((ROWS, 0),), half_span * block_size)
        lanes = -class_dev % 128
        extended = jnp.pad(extended, ((0, 0), (0, lanes)))
        product_sum = block_product(graph_tiles, local_col, tile_count, extended)
        applied = direction - damping * product_sum[:, :class_dev]
        curve_part = jnp.sum(direction * applied, axis=0)
        if norm_now is None:
            both = rows_sum(jnp.stack([jnp.sum(residual * residual, axis=0), curve_part]))
            norm_now, curve_sum = both[0], both[1]
        else:
            curve_sum = rows_sum(curve_part)
        step_size = norm_now / curve_sum
        solution = solution + step_size[None, :] * direction
        residual = residual - step_size[None, :] * applied
        norm_next = squares(residual)
        direction = residual + (norm_next / norm_now)[None, :] * direction
        norm_now = norm_next
    row_squares = cols_sum(jnp.sum(solution * solution, axis=1))
    length = jnp.sqrt(row_squares + 1e-06)
    return (solution / length[:, None], residual)


def factor(devices, pick):
    total = devices.shape[0]
    inner = len({pick(d) for d in devices})
    if inner < 1 or total % inner:
        return (1, total)
    return (total // inner, inner)


def solution(mesh):
    grid = mesh.devices
    row_shape = factor(grid[:, 0], lambda d: d.coords[2])
    col_shape = factor(grid[0, :], lambda d: d.core_on_chip)
    split = Mesh(grid.reshape(row_shape + col_shape), ROWS + COLS)
    placed = (
        P(ROWS, None, None, None),
        P(ROWS, None),
        P(ROWS),
        P(ROWS),
        P(ROWS),
        P(COLS),
    )
    return jax.shard_map(
        body,
        mesh=split,
        in_specs=placed,
        out_specs=(P(ROWS, COLS), P(ROWS, COLS)),
        check_vma=False,
    )
```

```python
import jax
import jax.numpy as jnp
from jax import lax
from jax.experimental import pallas as pl
from jax.experimental.pallas import tpu as pltpu
from jax.sharding import Mesh, PartitionSpec as P

ITERS = 3
ROWS = ("rx", "rz")
COLS = ("cy", "cc")


damping = 0.99
smoothing = 0.1


def padded(cells, sides, width):
    for axis, dim in sides:
        count = lax.axis_size(axis)
        head = lax.slice_in_dim(cells, 0, width, axis=dim)
        tail = lax.slice_in_dim(cells, cells.shape[dim] - width, cells.shape[dim], axis=dim)
        cells = jnp.concatenate(
            [
                lax.ppermute(tail, axis, [(i, (i + 1) % count) for i in range(count)]),
                cells,
                lax.ppermute(head, axis, [((i + 1) % count, i) for i in range(count)]),
            ],
            axis=dim,
        )
    return cells


def rows_sum(v):
    count = lax.axis_size(ROWS)
    spread = jnp.broadcast_to(v[None], (count,) + v.shape)
    gathered = lax.all_to_all(spread, ROWS, 0, 0, tiled=True)
    return jnp.sum(gathered, axis=0)


def cols_sum(v):
    return lax.psum(lax.psum(v, "cc"), "cy")


def tile_kernel(col_ref, count_ref, tile_ref, vec_ref, out_ref):
    step = pl.program_id(0)
    group, slots, size, _ = tile_ref.shape
    for inner in range(group):
        row = step * group + inner
        live = count_ref[row]
        lhs = jnp.concatenate([tile_ref[inner, slot] for slot in range(slots)], axis=1)
        pieces = []
        for slot in range(slots):
            start = pl.multiple_of(col_ref[row * slots + slot] * size, size)
            block = vec_ref[pl.ds(start, size), :]
            pieces.append(jnp.where(slot < live, block, jnp.zeros_like(block)))
        rhs = jnp.concatenate(pieces, axis=0)
        out_ref[pl.ds(inner * size, size), :] = jnp.dot(
            lhs, rhs, preferred_element_type=jnp.float32
        )


def block_product(graph_tiles, local_col, tile_count, extended):
    block_rows, slot_count, size, _ = graph_tiles.shape
    width = extended.shape[1]
    group = max(g for g in (1, 2, 4) if block_rows % g == 0)
    grid_spec = pltpu.PrefetchScalarGridSpec(
        num_scalar_prefetch=2,
        grid=(block_rows // group,),
        in_specs=[
            pl.BlockSpec((group, slot_count, size, size), lambda r, c, n: (r, 0, 0, 0)),
            pl.BlockSpec(extended.shape, lambda r, c, n: (0, 0)),
        ],
        out_specs=pl.BlockSpec((group * size, width), lambda r, c, n: (r, 0)),
    )
    cost = pl.CostEstimate(
        flops=2 * block_rows * slot_count * size * size * width,
        bytes_accessed=graph_tiles.size * 2 + extended.size * 2 + block_rows * size * width * 4,
        transcendentals=0,
    )
    return pl.pallas_call(
        tile_kernel,
        grid_spec=grid_spec,
        out_shape=jax.ShapeDtypeStruct((block_rows * size, width), jnp.float32),
        cost_estimate=cost,
    )(local_col.reshape(-1), tile_count, graph_tiles, extended)


def body(graph_tiles, tile_column, tile_count, class_label, confidence, class_weight):
    block_rows = graph_tiles.shape[0]
    slot_count = graph_tiles.shape[1]
    block_size = graph_tiles.shape[2]
    class_dev = class_weight.shape[0]
    half_span = block_rows // 2
    total_blocks = block_rows * lax.axis_size(ROWS)
    first_row = lax.axis_index(ROWS) * block_rows - half_span
    live_slot = jnp.arange(slot_count, dtype=jnp.int32)[None, :] < tile_count[:, None]
    local_col = jnp.where(live_slot, jnp.mod(tile_column - first_row, total_blocks), 0)
    class_ids = lax.axis_index(COLS) * class_dev + jnp.arange(class_dev, dtype=jnp.int32)
    onehot = (class_label[:, None] == class_ids[None, :]).astype(jnp.float32)
    prior_labels = (
        confidence[:, None]
        * class_weight[None, :]
        * ((1.0 - smoothing) * onehot + smoothing / (class_dev * lax.axis_size(COLS)))
    )

    def squares(residual):
        return rows_sum(jnp.sum(residual * residual, axis=0))

    solution = jnp.zeros_like(prior_labels)
    residual = prior_labels
    direction = prior_labels
    norm_now = None
    for step in range(ITERS):
        extended = padded(direction.astype(jnp.bfloat16), ((ROWS, 0),), half_span * block_size)
        lanes = -class_dev % 128
        extended = jnp.pad(extended, ((0, 0), (0, lanes)))
        product_sum = block_product(graph_tiles, local_col, tile_count, extended)
        applied = direction - damping * product_sum[:, :class_dev]
        curve_part = jnp.sum(direction * applied, axis=0)
        if norm_now is None:
            both = rows_sum(jnp.stack([jnp.sum(residual * residual, axis=0), curve_part]))
            norm_now, curve_sum = both[0], both[1]
        else:
            curve_sum = rows_sum(curve_part)
        step_size = norm_now / curve_sum
        solution = solution + step_size[None, :] * direction
        residual = residual - step_size[None, :] * applied
        norm_next = squares(residual)
        direction = residual + (norm_next / norm_now)[None, :] * direction
        norm_now = norm_next
    row_squares = cols_sum(jnp.sum(solution * solution, axis=1))
    length = jnp.sqrt(row_squares + 1e-06)
    return (solution / length[:, None], residual)


def factor(devices, pick):
    total = devices.shape[0]
    inner = len({pick(d) for d in devices})
    if inner < 1 or total % inner:
        return (1, total)
    return (total // inner, inner)


def solution(mesh):
    grid = mesh.devices
    row_shape = factor(grid[:, 0], lambda d: d.coords[2])
    col_shape = factor(grid[0, :], lambda d: d.core_on_chip)
    split = Mesh(grid.reshape(row_shape + col_shape), ROWS + COLS)
    placed = (
        P(ROWS, None, None, None),
        P(ROWS, None),
        P(ROWS),
        P(ROWS),
        P(ROWS),
        P(COLS),
    )
    return jax.shard_map(
        body,
        mesh=split,
        in_specs=placed,
        out_specs=(P(ROWS, COLS), P(ROWS, COLS)),
        check_vma=False,
    )
```

```python
import jax
import jax.numpy as jnp
from jax import lax
from jax.experimental import pallas as pl
from jax.experimental.pallas import tpu as pltpu
from jax.sharding import Mesh, PartitionSpec as P

ITERS = 3
ROWS = ("rx", "rz")
COLS = ("cy", "cc")


damping = 0.99
smoothing = 0.1


def padded(cells, sides, width):
    for axis, dim in sides:
        count = lax.axis_size(axis)
        head = lax.slice_in_dim(cells, 0, width, axis=dim)
        tail = lax.slice_in_dim(cells, cells.shape[dim] - width, cells.shape[dim], axis=dim)
        cells = jnp.concatenate(
            [
                lax.ppermute(tail, axis, [(i, (i + 1) % count) for i in range(count)]),
                cells,
                lax.ppermute(head, axis, [((i + 1) % count, i) for i in range(count)]),
            ],
            axis=dim,
        )
    return cells


def rows_sum(v):
    count = lax.axis_size(ROWS)
    spread = jnp.broadcast_to(v[None], (count,) + v.shape)
    gathered = lax.all_to_all(spread, ROWS, 0, 0, tiled=True)
    return jnp.sum(gathered, axis=0)


def cols_sum(v):
    return lax.psum(lax.psum(v, "cc"), "cy")


def tile_kernel(col_ref, count_ref, tile_ref, vec_ref, out_ref):
    step = pl.program_id(0)
    group, slots, size, _ = tile_ref.shape
    for inner in range(group):
        row = step * group + inner
        live = count_ref[row]
        lhs = jnp.concatenate([tile_ref[inner, slot] for slot in range(slots)], axis=1)
        pieces = []
        for slot in range(slots):
            start = pl.multiple_of(col_ref[row * slots + slot] * size, size)
            block = vec_ref[pl.ds(start, size), :]
            pieces.append(jnp.where(slot < live, block, jnp.zeros_like(block)))
        rhs = jnp.concatenate(pieces, axis=0)
        out_ref[pl.ds(inner * size, size), :] = jnp.dot(
            lhs, rhs, preferred_element_type=jnp.float32
        )


def block_product(graph_tiles, local_col, tile_count, extended):
    block_rows, slot_count, size, _ = graph_tiles.shape
    width = extended.shape[1]
    group = max(g for g in (1, 2, 4) if block_rows % g == 0)
    grid_spec = pltpu.PrefetchScalarGridSpec(
        num_scalar_prefetch=2,
        grid=(block_rows // group,),
        in_specs=[
            pl.BlockSpec((group, slot_count, size, size), lambda r, c, n: (r, 0, 0, 0)),
            pl.BlockSpec(extended.shape, lambda r, c, n: (0, 0)),
        ],
        out_specs=pl.BlockSpec((group * size, width), lambda r, c, n: (r, 0)),
    )
    cost = pl.CostEstimate(
        flops=2 * block_rows * slot_count * size * size * width,
        bytes_accessed=graph_tiles.size * 2 + extended.size * 2 + block_rows * size * width * 4,
        transcendentals=0,
    )
    return pl.pallas_call(
        tile_kernel,
        grid_spec=grid_spec,
        out_shape=jax.ShapeDtypeStruct((block_rows * size, width), jnp.float32),
        cost_estimate=cost,
    )(local_col.reshape(-1), tile_count, graph_tiles, extended)


def body(graph_tiles, tile_column, tile_count, class_label, confidence, class_weight):
    block_rows = graph_tiles.shape[0]
    slot_count = graph_tiles.shape[1]
    block_size = graph_tiles.shape[2]
    class_dev = class_weight.shape[0]
    half_span = block_rows // 2
    total_blocks = block_rows * lax.axis_size(ROWS)
    first_row = lax.axis_index(ROWS) * block_rows - half_span
    live_slot = jnp.arange(slot_count, dtype=jnp.int32)[None, :] < tile_count[:, None]
    local_col = jnp.where(live_slot, jnp.mod(tile_column - first_row, total_blocks), 0)
    class_ids = lax.axis_index(COLS) * class_dev + jnp.arange(class_dev, dtype=jnp.int32)
    halo_rows = half_span * block_size
    sides = ((ROWS, 0),)
    label_ext = padded(class_label, sides, halo_rows)
    confidence_ext = padded(confidence, sides, halo_rows)
    onehot = (label_ext[:, None] == class_ids[None, :]).astype(jnp.float32)
    prior_ext = (
        confidence_ext[:, None]
        * class_weight[None, :]
        * ((1.0 - smoothing) * onehot + smoothing / (class_dev * lax.axis_size(COLS)))
    )
    own = slice(halo_rows, halo_rows + block_rows * block_size)
    lanes = -class_dev % 128

    def squares(residual):
        return rows_sum(jnp.sum(residual * residual, axis=0))

    residual = prior_ext[own]
    direction_ext = prior_ext
    direction = residual
    solution = jnp.zeros_like(residual)
    norm_now = None
    for step in range(ITERS):
        extended = jnp.pad(direction_ext.astype(jnp.bfloat16), ((0, 0), (0, lanes)))
        product_sum = block_product(graph_tiles, local_col, tile_count, extended)
        applied = direction - damping * product_sum[:, :class_dev]
        curve_part = jnp.sum(direction * applied, axis=0)
        if norm_now is None:
            both = rows_sum(jnp.stack([jnp.sum(residual * residual, axis=0), curve_part]))
            norm_now, curve_sum = both[0], both[1]
        else:
            curve_sum = rows_sum(curve_part)
        step_size = norm_now / curve_sum
        solution = solution + step_size[None, :] * direction
        residual = residual - step_size[None, :] * applied
        residual_ext = padded(residual, sides, halo_rows)
        norm_next = squares(residual)
        direction_ext = residual_ext + (norm_next / norm_now)[None, :] * direction_ext
        direction = direction_ext[own]
        norm_now = norm_next
    row_squares = cols_sum(jnp.sum(solution * solution, axis=1))
    length = jnp.sqrt(row_squares + 1e-06)
    return (solution / length[:, None], residual)


def factor(devices, pick):
    total = devices.shape[0]
    inner = len({pick(d) for d in devices})
    if inner < 1 or total % inner:
        return (1, total)
    return (total // inner, inner)


def solution(mesh):
    grid = mesh.devices
    row_shape = factor(grid[:, 0], lambda d: d.coords[2])
    col_shape = factor(grid[0, :], lambda d: d.core_on_chip)
    split = Mesh(grid.reshape(row_shape + col_shape), ROWS + COLS)
    placed = (
        P(ROWS, None, None, None),
        P(ROWS, None),
        P(ROWS),
        P(ROWS),
        P(ROWS),
        P(COLS),
    )
    return jax.shard_map(
        body,
        mesh=split,
        in_specs=placed,
        out_specs=(P(ROWS, COLS), P(ROWS, COLS)),
        check_vma=False,
    )
```

```python
import jax
import jax.numpy as jnp
from jax import lax
from jax.experimental import pallas as pl
from jax.experimental.pallas import tpu as pltpu
from jax.sharding import Mesh, PartitionSpec as P

ITERS = 3
ROWS = ("rx", "rz")
COLS = ("cy", "cc")


damping = 0.99
smoothing = 0.1


def padded(cells, sides, width):
    for axis, dim in sides:
        count = lax.axis_size(axis)
        head = lax.slice_in_dim(cells, 0, width, axis=dim)
        tail = lax.slice_in_dim(cells, cells.shape[dim] - width, cells.shape[dim], axis=dim)
        cells = jnp.concatenate(
            [
                lax.ppermute(tail, axis, [(i, (i + 1) % count) for i in range(count)]),
                cells,
                lax.ppermute(head, axis, [((i + 1) % count, i) for i in range(count)]),
            ],
            axis=dim,
        )
    return cells


def rows_sum(v):
    count = lax.axis_size(ROWS)
    spread = jnp.broadcast_to(v[None], (count,) + v.shape)
    gathered = lax.all_to_all(spread, ROWS, 0, 0, tiled=True)
    return jnp.sum(gathered, axis=0)


def cols_sum(v):
    count = lax.axis_size(COLS)
    spread = jnp.broadcast_to(v[None], (count,) + v.shape)
    gathered = lax.all_to_all(spread, COLS, 0, 0, tiled=True)
    return jnp.sum(gathered, axis=0)


def tile_kernel(col_ref, count_ref, tile_ref, vec_ref, out_ref):
    step = pl.program_id(0)
    group, slots, size, _ = tile_ref.shape
    for inner in range(group):
        row = step * group + inner
        live = count_ref[row]
        lhs = jnp.concatenate([tile_ref[inner, slot] for slot in range(slots)], axis=1)
        pieces = []
        for slot in range(slots):
            start = pl.multiple_of(col_ref[row * slots + slot] * size, size)
            block = vec_ref[pl.ds(start, size), :]
            pieces.append(jnp.where(slot < live, block, jnp.zeros_like(block)))
        rhs = jnp.concatenate(pieces, axis=0)
        out_ref[pl.ds(inner * size, size), :] = jnp.dot(
            lhs, rhs, preferred_element_type=jnp.float32
        )


def block_product(graph_tiles, local_col, tile_count, extended):
    block_rows, slot_count, size, _ = graph_tiles.shape
    width = extended.shape[1]
    group = max(g for g in (1, 2, 4) if block_rows % g == 0)
    grid_spec = pltpu.PrefetchScalarGridSpec(
        num_scalar_prefetch=2,
        grid=(block_rows // group,),
        in_specs=[
            pl.BlockSpec((group, slot_count, size, size), lambda r, c, n: (r, 0, 0, 0)),
            pl.BlockSpec(extended.shape, lambda r, c, n: (0, 0)),
        ],
        out_specs=pl.BlockSpec((group * size, width), lambda r, c, n: (r, 0)),
    )
    cost = pl.CostEstimate(
        flops=2 * block_rows * slot_count * size * size * width,
        bytes_accessed=graph_tiles.size * 2 + extended.size * 2 + block_rows * size * width * 4,
        transcendentals=0,
    )
    return pl.pallas_call(
        tile_kernel,
        grid_spec=grid_spec,
        out_shape=jax.ShapeDtypeStruct((block_rows * size, width), jnp.float32),
        cost_estimate=cost,
    )(local_col.reshape(-1), tile_count, graph_tiles, extended)


def body(graph_tiles, tile_column, tile_count, class_label, confidence, class_weight):
    block_rows = graph_tiles.shape[0]
    slot_count = graph_tiles.shape[1]
    block_size = graph_tiles.shape[2]
    class_dev = class_weight.shape[0]
    half_span = block_rows // 2
    total_blocks = block_rows * lax.axis_size(ROWS)
    first_row = lax.axis_index(ROWS) * block_rows - half_span
    live_slot = jnp.arange(slot_count, dtype=jnp.int32)[None, :] < tile_count[:, None]
    local_col = jnp.where(live_slot, jnp.mod(tile_column - first_row, total_blocks), 0)
    class_ids = lax.axis_index(COLS) * class_dev + jnp.arange(class_dev, dtype=jnp.int32)
    halo_rows = half_span * block_size
    sides = ((ROWS, 0),)
    packed = jnp.stack([class_label.astype(jnp.float32), confidence])
    packed_ext = padded(packed, ((ROWS, 1),), halo_rows)
    label_ext = packed_ext[0].astype(jnp.int32)
    confidence_ext = packed_ext[1]
    onehot = (label_ext[:, None] == class_ids[None, :]).astype(jnp.float32)
    prior_ext = (
        confidence_ext[:, None]
        * class_weight[None, :]
        * ((1.0 - smoothing) * onehot + smoothing / (class_dev * lax.axis_size(COLS)))
    )
    own = slice(halo_rows, halo_rows + block_rows * block_size)
    lanes = -class_dev % 128

    def squares(residual):
        return rows_sum(jnp.sum(residual * residual, axis=0))

    residual = prior_ext[own]
    direction_ext = prior_ext
    direction = residual
    solution = jnp.zeros_like(residual)
    norm_now = None
    for step in range(ITERS):
        extended = jnp.pad(direction_ext.astype(jnp.bfloat16), ((0, 0), (0, lanes)))
        product_sum = block_product(graph_tiles, local_col, tile_count, extended)
        applied = direction - damping * product_sum[:, :class_dev]
        curve_part = jnp.sum(direction * applied, axis=0)
        if norm_now is None:
            both = rows_sum(jnp.stack([jnp.sum(residual * residual, axis=0), curve_part]))
            norm_now, curve_sum = both[0], both[1]
        else:
            curve_sum = rows_sum(curve_part)
        step_size = norm_now / curve_sum
        solution = solution + step_size[None, :] * direction
        residual = residual - step_size[None, :] * applied
        residual_ext = padded(residual, sides, halo_rows)
        norm_next = squares(residual)
        direction_ext = residual_ext + (norm_next / norm_now)[None, :] * direction_ext
        direction = direction_ext[own]
        norm_now = norm_next
    row_squares = cols_sum(jnp.sum(solution * solution, axis=1))
    length = jnp.sqrt(row_squares + 1e-06)
    return (solution / length[:, None], residual)


def factor(devices, pick):
    total = devices.shape[0]
    inner = len({pick(d) for d in devices})
    if inner < 1 or total % inner:
        return (1, total)
    return (total // inner, inner)


def solution(mesh):
    grid = mesh.devices
    row_shape = factor(grid[:, 0], lambda d: d.coords[2])
    col_shape = factor(grid[0, :], lambda d: d.core_on_chip)
    split = Mesh(grid.reshape(row_shape + col_shape), ROWS + COLS)
    placed = (
        P(ROWS, None, None, None),
        P(ROWS, None),
        P(ROWS),
        P(ROWS),
        P(ROWS),
        P(COLS),
    )
    return jax.shard_map(
        body,
        mesh=split,
        in_specs=placed,
        out_specs=(P(ROWS, COLS), P(ROWS, COLS)),
        check_vma=False,
    )
```

```python
import jax
import jax.numpy as jnp
from jax import lax
from jax.experimental import pallas as pl
from jax.experimental.pallas import tpu as pltpu
from jax.sharding import Mesh, PartitionSpec as P

ITERS = 3
ROWS = ("rx", "rz")
COLS = ("cy", "cc")


damping = 0.99
smoothing = 0.1


def padded(cells, sides, width):
    for axis, dim in sides:
        count = lax.axis_size(axis)
        head = lax.slice_in_dim(cells, 0, width, axis=dim)
        tail = lax.slice_in_dim(cells, cells.shape[dim] - width, cells.shape[dim], axis=dim)
        cells = jnp.concatenate(
            [
                lax.ppermute(tail, axis, [(i, (i + 1) % count) for i in range(count)]),
                cells,
                lax.ppermute(head, axis, [((i + 1) % count, i) for i in range(count)]),
            ],
            axis=dim,
        )
    return cells


def rows_sum(v):
    count = lax.axis_size(ROWS)
    spread = jnp.broadcast_to(v[None], (count,) + v.shape)
    gathered = lax.all_to_all(spread, ROWS, 0, 0, tiled=True)
    return jnp.sum(gathered, axis=0)


def cols_sum(v):
    count = lax.axis_size(COLS)
    spread = jnp.broadcast_to(v[None], (count,) + v.shape)
    gathered = lax.all_to_all(spread, COLS, 0, 0, tiled=True)
    return jnp.sum(gathered, axis=0)


def tile_kernel(col_ref, count_ref, tile_ref, vec_ref, out_ref):
    step = pl.program_id(0)
    group, slots, size, _ = tile_ref.shape
    for inner in range(group):
        row = step * group + inner
        live = count_ref[row]
        lhs = jnp.concatenate([tile_ref[inner, slot] for slot in range(slots)], axis=1)
        pieces = []
        for slot in range(slots):
            start = pl.multiple_of(col_ref[row * slots + slot] * size, size)
            block = vec_ref[pl.ds(start, size), :]
            pieces.append(jnp.where(slot < live, block, jnp.zeros_like(block)))
        rhs = jnp.concatenate(pieces, axis=0)
        out_ref[pl.ds(inner * size, size), :] = jnp.dot(
            lhs, rhs, preferred_element_type=jnp.float32
        )


def block_product(graph_tiles, local_col, tile_count, extended):
    block_rows, slot_count, size, _ = graph_tiles.shape
    width = extended.shape[1]
    group = max(g for g in (1, 2, 4) if block_rows % g == 0)
    grid_spec = pltpu.PrefetchScalarGridSpec(
        num_scalar_prefetch=2,
        grid=(block_rows // group,),
        in_specs=[
            pl.BlockSpec((group, slot_count, size, size), lambda r, c, n: (r, 0, 0, 0)),
            pl.BlockSpec(extended.shape, lambda r, c, n: (0, 0)),
        ],
        out_specs=pl.BlockSpec((group * size, width), lambda r, c, n: (r, 0)),
    )
    cost = pl.CostEstimate(
        flops=2 * block_rows * slot_count * size * size * width,
        bytes_accessed=graph_tiles.size * 2 + extended.size * 2 + block_rows * size * width * 4,
        transcendentals=0,
    )
    return pl.pallas_call(
        tile_kernel,
        grid_spec=grid_spec,
        out_shape=jax.ShapeDtypeStruct((block_rows * size, width), jnp.float32),
        cost_estimate=cost,
    )(local_col.reshape(-1), tile_count, graph_tiles, extended)


def body(graph_tiles, tile_column, tile_count, class_label, confidence, class_weight):
    block_rows = graph_tiles.shape[0]
    slot_count = graph_tiles.shape[1]
    block_size = graph_tiles.shape[2]
    class_dev = class_weight.shape[0]
    half_span = block_rows // 2
    total_blocks = block_rows * lax.axis_size(ROWS)
    first_row = lax.axis_index(ROWS) * block_rows - half_span
    live_slot = jnp.arange(slot_count, dtype=jnp.int32)[None, :] < tile_count[:, None]
    local_col = jnp.where(live_slot, jnp.mod(tile_column - first_row, total_blocks), 0)
    class_ids = lax.axis_index(COLS) * class_dev + jnp.arange(class_dev, dtype=jnp.int32)
    halo_rows = half_span * block_size
    sides = ((ROWS, 0),)
    packed = jnp.stack([class_label.astype(jnp.float32), confidence])
    packed_ext = padded(packed, ((ROWS, 1),), halo_rows)
    label_ext = packed_ext[0].astype(jnp.int32)
    confidence_ext = packed_ext[1]
    onehot = (label_ext[:, None] == class_ids[None, :]).astype(jnp.float32)
    prior_ext = (
        confidence_ext[:, None]
        * class_weight[None, :]
        * ((1.0 - smoothing) * onehot + smoothing / (class_dev * lax.axis_size(COLS)))
    )
    own = slice(halo_rows, halo_rows + block_rows * block_size)

    def squares(residual):
        return rows_sum(jnp.sum(residual * residual, axis=0))

    residual = prior_ext[own]
    direction_ext = prior_ext
    direction = residual
    solution = jnp.zeros_like(residual)
    norm_now = None
    for step in range(ITERS):
        extended = direction_ext.astype(jnp.bfloat16)
        product_sum = block_product(graph_tiles, local_col, tile_count, extended)
        applied = direction - damping * product_sum
        curve_part = jnp.sum(direction * applied, axis=0)
        if norm_now is None:
            both = rows_sum(jnp.stack([jnp.sum(residual * residual, axis=0), curve_part]))
            norm_now, curve_sum = both[0], both[1]
        else:
            curve_sum = rows_sum(curve_part)
        step_size = norm_now / curve_sum
        solution = solution + step_size[None, :] * direction
        residual = residual - step_size[None, :] * applied
        residual_ext = padded(residual, sides, halo_rows)
        norm_next = squares(residual)
        direction_ext = residual_ext + (norm_next / norm_now)[None, :] * direction_ext
        direction = direction_ext[own]
        norm_now = norm_next
    row_squares = cols_sum(jnp.sum(solution * solution, axis=1))
    length = jnp.sqrt(row_squares + 1e-06)
    return (solution / length[:, None], residual)


def factor(devices, pick):
    total = devices.shape[0]
    inner = len({pick(d) for d in devices})
    if inner < 1 or total % inner:
        return (1, total)
    return (total // inner, inner)


def solution(mesh):
    grid = mesh.devices
    row_shape = factor(grid[:, 0], lambda d: d.coords[2])
    col_shape = factor(grid[0, :], lambda d: d.core_on_chip)
    split = Mesh(grid.reshape(row_shape + col_shape), ROWS + COLS)
    placed = (
        P(ROWS, None, None, None),
        P(ROWS, None),
        P(ROWS),
        P(ROWS),
        P(ROWS),
        P(COLS),
    )
    return jax.shard_map(
        body,
        mesh=split,
        in_specs=placed,
        out_specs=(P(ROWS, COLS), P(ROWS, COLS)),
        check_vma=False,
    )
```

```python
import jax
import jax.numpy as jnp
from jax import lax
from jax.experimental import pallas as pl
from jax.experimental.pallas import tpu as pltpu
from jax.sharding import Mesh, PartitionSpec as P

ITERS = 3
ROWS = ("rx", "rz")
COLS = ("cy", "cc")


damping = 0.99
smoothing = 0.1


def padded(cells, sides, width):
    for axis, dim in sides:
        count = lax.axis_size(axis)
        head = lax.slice_in_dim(cells, 0, width, axis=dim)
        tail = lax.slice_in_dim(cells, cells.shape[dim] - width, cells.shape[dim], axis=dim)
        cells = jnp.concatenate(
            [
                lax.ppermute(tail, axis, [(i, (i + 1) % count) for i in range(count)]),
                cells,
                lax.ppermute(head, axis, [((i + 1) % count, i) for i in range(count)]),
            ],
            axis=dim,
        )
    return cells


def rows_sum(v):
    count = lax.axis_size(ROWS)
    spread = jnp.broadcast_to(v[None], (count,) + v.shape)
    gathered = lax.all_to_all(spread, ROWS, 0, 0, tiled=True)
    return jnp.sum(gathered, axis=0)


def cols_sum(v):
    count = lax.axis_size(COLS)
    spread = jnp.broadcast_to(v[None], (count,) + v.shape)
    gathered = lax.all_to_all(spread, COLS, 0, 0, tiled=True)
    return jnp.sum(gathered, axis=0)


def tile_kernel(col_ref, count_ref, tile_ref, left_ref, mid_ref, right_ref, out_ref, vec_ref):
    step = pl.program_id(0)
    group, slots, size, _ = tile_ref.shape
    head = left_ref.shape[0]
    middle = mid_ref.shape[0]

    @pl.when(step == 0)
    def _():
        vec_ref[pl.ds(0, head), :] = left_ref[...]
        vec_ref[pl.ds(head, middle), :] = mid_ref[...]
        vec_ref[pl.ds(head + middle, right_ref.shape[0]), :] = right_ref[...]

    for inner in range(group):
        row = step * group + inner
        live = count_ref[row]
        lhs = jnp.concatenate([tile_ref[inner, slot] for slot in range(slots)], axis=1)
        pieces = []
        for slot in range(slots):
            start = pl.multiple_of(col_ref[row * slots + slot] * size, size)
            block = vec_ref[pl.ds(start, size), :]
            pieces.append(jnp.where(slot < live, block, jnp.zeros_like(block)))
        rhs = jnp.concatenate(pieces, axis=0)
        out_ref[pl.ds(inner * size, size), :] = jnp.dot(
            lhs, rhs, preferred_element_type=jnp.float32
        )


def block_product(graph_tiles, local_col, tile_count, left, middle, right):
    block_rows, slot_count, size, _ = graph_tiles.shape
    width = middle.shape[1]
    total = left.shape[0] + middle.shape[0] + right.shape[0]
    group = max(g for g in (1, 2, 4) if block_rows % g == 0)
    whole = lambda r, c, n: (0, 0)
    grid_spec = pltpu.PrefetchScalarGridSpec(
        num_scalar_prefetch=2,
        grid=(block_rows // group,),
        in_specs=[
            pl.BlockSpec((group, slot_count, size, size), lambda r, c, n: (r, 0, 0, 0)),
            pl.BlockSpec(left.shape, whole),
            pl.BlockSpec(middle.shape, whole),
            pl.BlockSpec(right.shape, whole),
        ],
        out_specs=pl.BlockSpec((group * size, width), lambda r, c, n: (r, 0)),
        scratch_shapes=[pltpu.VMEM((total, width), middle.dtype)],
    )
    cost = pl.CostEstimate(
        flops=2 * block_rows * slot_count * size * size * width,
        bytes_accessed=graph_tiles.size * 2 + total * width * 2 + block_rows * size * width * 4,
        transcendentals=0,
    )
    return pl.pallas_call(
        tile_kernel,
        grid_spec=grid_spec,
        out_shape=jax.ShapeDtypeStruct((block_rows * size, width), jnp.float32),
        cost_estimate=cost,
    )(local_col.reshape(-1), tile_count, graph_tiles, left, middle, right)


def halos(cells, axis, width, dim):
    count = lax.axis_size(axis)
    head = lax.slice_in_dim(cells, 0, width, axis=dim)
    tail = lax.slice_in_dim(cells, cells.shape[dim] - width, cells.shape[dim], axis=dim)
    left = lax.ppermute(tail, axis, [(i, (i + 1) % count) for i in range(count)])
    right = lax.ppermute(head, axis, [((i + 1) % count, i) for i in range(count)])
    return left, right


def body(graph_tiles, tile_column, tile_count, class_label, confidence, class_weight):
    block_rows = graph_tiles.shape[0]
    slot_count = graph_tiles.shape[1]
    block_size = graph_tiles.shape[2]
    class_dev = class_weight.shape[0]
    half_span = block_rows // 2
    total_blocks = block_rows * lax.axis_size(ROWS)
    first_row = lax.axis_index(ROWS) * block_rows - half_span
    live_slot = jnp.arange(slot_count, dtype=jnp.int32)[None, :] < tile_count[:, None]
    local_col = jnp.where(live_slot, jnp.mod(tile_column - first_row, total_blocks), 0)
    class_ids = lax.axis_index(COLS) * class_dev + jnp.arange(class_dev, dtype=jnp.int32)
    halo_rows = half_span * block_size
    spread = smoothing / (class_dev * lax.axis_size(COLS))

    def prior_of(label, weight):
        onehot = (label[:, None] == class_ids[None, :]).astype(jnp.float32)
        return weight[:, None] * class_weight[None, :] * ((1.0 - smoothing) * onehot + spread)

    packed = jnp.stack([class_label.astype(jnp.float32), confidence])
    left_pack, right_pack = halos(packed, ROWS, halo_rows, 1)
    left_dir = prior_of(left_pack[0].astype(jnp.int32), left_pack[1])
    right_dir = prior_of(right_pack[0].astype(jnp.int32), right_pack[1])

    def squares(residual):
        return rows_sum(jnp.sum(residual * residual, axis=0))

    residual = prior_of(class_label, confidence)
    direction = residual
    solution = jnp.zeros_like(residual)
    norm_now = None
    for step in range(ITERS):
        product_sum = block_product(
            graph_tiles,
            local_col,
            tile_count,
            left_dir.astype(jnp.bfloat16),
            direction.astype(jnp.bfloat16),
            right_dir.astype(jnp.bfloat16),
        )
        applied = direction - damping * product_sum
        curve_part = jnp.sum(direction * applied, axis=0)
        if norm_now is None:
            both = rows_sum(jnp.stack([jnp.sum(residual * residual, axis=0), curve_part]))
            norm_now, curve_sum = both[0], both[1]
        else:
            curve_sum = rows_sum(curve_part)
        step_size = norm_now / curve_sum
        solution = solution + step_size[None, :] * direction
        residual = residual - step_size[None, :] * applied
        left_res, right_res = halos(residual, ROWS, halo_rows, 0)
        norm_next = squares(residual)
        ratio = (norm_next / norm_now)[None, :]
        direction = residual + ratio * direction
        left_dir = left_res + ratio * left_dir
        right_dir = right_res + ratio * right_dir
        norm_now = norm_next
    row_squares = cols_sum(jnp.sum(solution * solution, axis=1))
    length = jnp.sqrt(row_squares + 1e-06)
    return (solution / length[:, None], residual)


def factor(devices, pick):
    total = devices.shape[0]
    inner = len({pick(d) for d in devices})
    if inner < 1 or total % inner:
        return (1, total)
    return (total // inner, inner)


def solution(mesh):
    grid = mesh.devices
    row_shape = factor(grid[:, 0], lambda d: d.coords[2])
    col_shape = factor(grid[0, :], lambda d: d.core_on_chip)
    split = Mesh(grid.reshape(row_shape + col_shape), ROWS + COLS)
    placed = (
        P(ROWS, None, None, None),
        P(ROWS, None),
        P(ROWS),
        P(ROWS),
        P(ROWS),
        P(COLS),
    )
    return jax.shard_map(
        body,
        mesh=split,
        in_specs=placed,
        out_specs=(P(ROWS, COLS), P(ROWS, COLS)),
        check_vma=False,
    )
```

```python
import jax
import jax.numpy as jnp
from jax import lax
from jax.experimental import pallas as pl
from jax.experimental.pallas import tpu as pltpu
from jax.sharding import Mesh, PartitionSpec as P

ITERS = 3
ROWS = ("rx", "rz")
COLS = ("cy", "cc")


damping = 0.99
smoothing = 0.1


def padded(cells, sides, width):
    for axis, dim in sides:
        count = lax.axis_size(axis)
        head = lax.slice_in_dim(cells, 0, width, axis=dim)
        tail = lax.slice_in_dim(cells, cells.shape[dim] - width, cells.shape[dim], axis=dim)
        cells = jnp.concatenate(
            [
                lax.ppermute(tail, axis, [(i, (i + 1) % count) for i in range(count)]),
                cells,
                lax.ppermute(head, axis, [((i + 1) % count, i) for i in range(count)]),
            ],
            axis=dim,
        )
    return cells


def rows_sum(v):
    count = lax.axis_size(ROWS)
    spread = jnp.broadcast_to(v[None], (count,) + v.shape)
    gathered = lax.all_to_all(spread, ROWS, 0, 0, tiled=True)
    return jnp.sum(gathered, axis=0)


def cols_sum(v):
    count = lax.axis_size(COLS)
    spread = jnp.broadcast_to(v[None], (count,) + v.shape)
    gathered = lax.all_to_all(spread, COLS, 0, 0, tiled=True)
    return jnp.sum(gathered, axis=0)


def tile_kernel(col_ref, count_ref, tile_ref, left_ref, mid_ref, right_ref, out_ref, vec_ref):
    step = pl.program_id(0)
    group, slots, size, _ = tile_ref.shape
    head = left_ref.shape[0]
    middle = mid_ref.shape[0]

    @pl.when(step == 0)
    def _():
        vec_ref[pl.ds(0, head), :] = left_ref[...]
        vec_ref[pl.ds(head, middle), :] = mid_ref[...]
        vec_ref[pl.ds(head + middle, right_ref.shape[0]), :] = right_ref[...]

    for inner in range(group):
        row = step * group + inner
        live = count_ref[row]
        lhs = jnp.concatenate([tile_ref[inner, slot] for slot in range(slots)], axis=1)
        pieces = []
        for slot in range(slots):
            start = pl.multiple_of(col_ref[row * slots + slot] * size, size)
            block = vec_ref[pl.ds(start, size), :]
            pieces.append(jnp.where(slot < live, block, jnp.zeros_like(block)))
        rhs = jnp.concatenate(pieces, axis=0)
        out_ref[pl.ds(inner * size, size), :] = jnp.dot(
            lhs, rhs, preferred_element_type=jnp.float32
        )


def block_product(graph_tiles, local_col, tile_count, left, middle, right):
    block_rows, slot_count, size, _ = graph_tiles.shape
    width = middle.shape[1]
    total = left.shape[0] + middle.shape[0] + right.shape[0]
    group = max(g for g in (1, 2, 4, 8) if block_rows % g == 0)
    whole = lambda r, c, n: (0, 0)
    grid_spec = pltpu.PrefetchScalarGridSpec(
        num_scalar_prefetch=2,
        grid=(block_rows // group,),
        in_specs=[
            pl.BlockSpec((group, slot_count, size, size), lambda r, c, n: (r, 0, 0, 0)),
            pl.BlockSpec(left.shape, whole),
            pl.BlockSpec(middle.shape, whole),
            pl.BlockSpec(right.shape, whole),
        ],
        out_specs=pl.BlockSpec((group * size, width), lambda r, c, n: (r, 0)),
        scratch_shapes=[pltpu.VMEM((total, width), middle.dtype)],
    )
    cost = pl.CostEstimate(
        flops=2 * block_rows * slot_count * size * size * width,
        bytes_accessed=graph_tiles.size * 2 + total * width * 2 + block_rows * size * width * 4,
        transcendentals=0,
    )
    return pl.pallas_call(
        tile_kernel,
        grid_spec=grid_spec,
        out_shape=jax.ShapeDtypeStruct((block_rows * size, width), jnp.float32),
        cost_estimate=cost,
    )(local_col.reshape(-1), tile_count, graph_tiles, left, middle, right)


def halos(cells, axis, width, dim):
    count = lax.axis_size(axis)
    head = lax.slice_in_dim(cells, 0, width, axis=dim)
    tail = lax.slice_in_dim(cells, cells.shape[dim] - width, cells.shape[dim], axis=dim)
    left = lax.ppermute(tail, axis, [(i, (i + 1) % count) for i in range(count)])
    right = lax.ppermute(head, axis, [((i + 1) % count, i) for i in range(count)])
    return left, right


def body(graph_tiles, tile_column, tile_count, class_label, confidence, class_weight):
    block_rows = graph_tiles.shape[0]
    slot_count = graph_tiles.shape[1]
    block_size = graph_tiles.shape[2]
    class_dev = class_weight.shape[0]
    half_span = block_rows // 2
    total_blocks = block_rows * lax.axis_size(ROWS)
    first_row = lax.axis_index(ROWS) * block_rows - half_span
    live_slot = jnp.arange(slot_count, dtype=jnp.int32)[None, :] < tile_count[:, None]
    local_col = jnp.where(live_slot, jnp.mod(tile_column - first_row, total_blocks), 0)
    class_ids = lax.axis_index(COLS) * class_dev + jnp.arange(class_dev, dtype=jnp.int32)
    halo_rows = half_span * block_size
    spread = smoothing / (class_dev * lax.axis_size(COLS))

    def prior_of(label, weight):
        onehot = (label[:, None] == class_ids[None, :]).astype(jnp.float32)
        return weight[:, None] * class_weight[None, :] * ((1.0 - smoothing) * onehot + spread)

    packed = jnp.stack([class_label.astype(jnp.float32), confidence])
    left_pack, right_pack = halos(packed, ROWS, halo_rows, 1)
    left_dir = prior_of(left_pack[0].astype(jnp.int32), left_pack[1])
    right_dir = prior_of(right_pack[0].astype(jnp.int32), right_pack[1])

    def squares(residual):
        return rows_sum(jnp.sum(residual * residual, axis=0))

    residual = prior_of(class_label, confidence)
    direction = residual
    left_res, right_res = left_dir, right_dir
    solution = jnp.zeros_like(residual)
    norm_now = None
    for step in range(ITERS):
        product_sum = block_product(
            graph_tiles,
            local_col,
            tile_count,
            left_dir.astype(jnp.bfloat16),
            direction.astype(jnp.bfloat16),
            right_dir.astype(jnp.bfloat16),
        )
        applied = direction - damping * product_sum
        left_app, right_app = halos(applied, ROWS, halo_rows, 0)
        curve_part = jnp.sum(direction * applied, axis=0)
        if norm_now is None:
            both = rows_sum(jnp.stack([jnp.sum(residual * residual, axis=0), curve_part]))
            norm_now, curve_sum = both[0], both[1]
        else:
            curve_sum = rows_sum(curve_part)
        step_size = norm_now / curve_sum
        solution = solution + step_size[None, :] * direction
        residual = residual - step_size[None, :] * applied
        left_res = left_res - step_size[None, :] * left_app
        right_res = right_res - step_size[None, :] * right_app
        norm_next = squares(residual)
        ratio = (norm_next / norm_now)[None, :]
        direction = residual + ratio * direction
        left_dir = left_res + ratio * left_dir
        right_dir = right_res + ratio * right_dir
        norm_now = norm_next
    row_squares = cols_sum(jnp.sum(solution * solution, axis=1))
    length = jnp.sqrt(row_squares + 1e-06)
    return (solution / length[:, None], residual)


def factor(devices, pick):
    total = devices.shape[0]
    inner = len({pick(d) for d in devices})
    if inner < 1 or total % inner:
        return (1, total)
    return (total // inner, inner)


def solution(mesh):
    grid = mesh.devices
    row_shape = factor(grid[:, 0], lambda d: d.coords[2])
    col_shape = factor(grid[0, :], lambda d: d.core_on_chip)
    split = Mesh(grid.reshape(row_shape + col_shape), ROWS + COLS)
    placed = (
        P(ROWS, None, None, None),
        P(ROWS, None),
        P(ROWS),
        P(ROWS),
        P(ROWS),
        P(COLS),
    )
    return jax.shard_map(
        body,
        mesh=split,
        in_specs=placed,
        out_specs=(P(ROWS, COLS), P(ROWS, COLS)),
        check_vma=False,
    )
```

```python
import jax
import jax.numpy as jnp
from jax import lax
from jax.experimental import pallas as pl
from jax.experimental.pallas import tpu as pltpu
from jax.sharding import Mesh, PartitionSpec as P

ITERS = 3
ROWS = ("rx", "rz")
COLS = ("cy", "cc")


damping = 0.99
smoothing = 0.1


def padded(cells, sides, width):
    for axis, dim in sides:
        count = lax.axis_size(axis)
        head = lax.slice_in_dim(cells, 0, width, axis=dim)
        tail = lax.slice_in_dim(cells, cells.shape[dim] - width, cells.shape[dim], axis=dim)
        cells = jnp.concatenate(
            [
                lax.ppermute(tail, axis, [(i, (i + 1) % count) for i in range(count)]),
                cells,
                lax.ppermute(head, axis, [((i + 1) % count, i) for i in range(count)]),
            ],
            axis=dim,
        )
    return cells


def rows_sum(v):
    count = lax.axis_size(ROWS)
    spread = jnp.broadcast_to(v[None], (count,) + v.shape)
    gathered = lax.all_to_all(spread, ROWS, 0, 0, tiled=True)
    return jnp.sum(gathered, axis=0)


def cols_sum(v):
    count = lax.axis_size(COLS)
    spread = jnp.broadcast_to(v[None], (count,) + v.shape)
    gathered = lax.all_to_all(spread, COLS, 0, 0, tiled=True)
    return jnp.sum(gathered, axis=0)


def tile_kernel(col_ref, count_ref, tile_ref, left_ref, mid_ref, right_ref, out_ref, vec_ref):
    step = pl.program_id(0)
    group, slots, size, _ = tile_ref.shape
    head = left_ref.shape[0]
    middle = mid_ref.shape[0]

    @pl.when(step == 0)
    def _():
        vec_ref[pl.ds(0, head), :] = left_ref[...]
        vec_ref[pl.ds(head, middle), :] = mid_ref[...]
        vec_ref[pl.ds(head + middle, right_ref.shape[0]), :] = right_ref[...]

    for inner in range(group):
        row = step * group + inner
        live = count_ref[row]
        lhs = jnp.concatenate([tile_ref[inner, slot] for slot in range(slots)], axis=1)
        pieces = []
        for slot in range(slots):
            start = pl.multiple_of(col_ref[row * slots + slot] * size, size)
            block = vec_ref[pl.ds(start, size), :]
            pieces.append(jnp.where(slot < live, block, jnp.zeros_like(block)))
        rhs = jnp.concatenate(pieces, axis=0)
        out_ref[pl.ds(inner * size, size), :] = jnp.dot(
            lhs, rhs, preferred_element_type=jnp.float32
        )


def block_product(graph_tiles, local_col, tile_count, left, middle, right):
    block_rows, slot_count, size, _ = graph_tiles.shape
    width = middle.shape[1]
    total = left.shape[0] + middle.shape[0] + right.shape[0]
    group = max(g for g in (1, 2, 4, 8) if block_rows % g == 0)
    whole = lambda r, c, n: (0, 0)
    grid_spec = pltpu.PrefetchScalarGridSpec(
        num_scalar_prefetch=2,
        grid=(block_rows // group,),
        in_specs=[
            pl.BlockSpec((group, slot_count, size, size), lambda r, c, n: (r, 0, 0, 0)),
            pl.BlockSpec(left.shape, whole),
            pl.BlockSpec(middle.shape, whole),
            pl.BlockSpec(right.shape, whole),
        ],
        out_specs=pl.BlockSpec((group * size, width), lambda r, c, n: (r, 0)),
        scratch_shapes=[pltpu.VMEM((total, width), middle.dtype)],
    )
    cost = pl.CostEstimate(
        flops=2 * block_rows * slot_count * size * size * width,
        bytes_accessed=graph_tiles.size * 2 + total * width * 2 + block_rows * size * width * 4,
        transcendentals=0,
    )
    return pl.pallas_call(
        tile_kernel,
        grid_spec=grid_spec,
        out_shape=jax.ShapeDtypeStruct((block_rows * size, width), jnp.float32),
        cost_estimate=cost,
    )(local_col.reshape(-1), tile_count, graph_tiles, left, middle, right)


def halos(cells, axis, width, dim):
    count = lax.axis_size(axis)
    head = lax.slice_in_dim(cells, 0, width, axis=dim)
    tail = lax.slice_in_dim(cells, cells.shape[dim] - width, cells.shape[dim], axis=dim)
    left = lax.ppermute(tail, axis, [(i, (i + 1) % count) for i in range(count)])
    right = lax.ppermute(head, axis, [((i + 1) % count, i) for i in range(count)])
    return left, right


def body(graph_tiles, tile_column, tile_count, class_label, confidence, class_weight):
    block_rows = graph_tiles.shape[0]
    slot_count = graph_tiles.shape[1]
    block_size = graph_tiles.shape[2]
    class_dev = class_weight.shape[0]
    half_span = block_rows // 2
    total_blocks = block_rows * lax.axis_size(ROWS)
    first_row = lax.axis_index(ROWS) * block_rows - half_span
    live_slot = jnp.arange(slot_count, dtype=jnp.int32)[None, :] < tile_count[:, None]
    local_col = jnp.where(live_slot, jnp.mod(tile_column - first_row, total_blocks), 0)
    class_ids = lax.axis_index(COLS) * class_dev + jnp.arange(class_dev, dtype=jnp.int32)
    halo_rows = half_span * block_size
    spread = smoothing / (class_dev * lax.axis_size(COLS))

    def prior_of(label, weight):
        onehot = (label[:, None] == class_ids[None, :]).astype(jnp.float32)
        return weight[:, None] * class_weight[None, :] * ((1.0 - smoothing) * onehot + spread)

    packed = jnp.stack([class_label.astype(jnp.float32), confidence])
    left_pack, right_pack = halos(packed, ROWS, halo_rows, 1)
    left_dir = prior_of(left_pack[0].astype(jnp.int32), left_pack[1])
    right_dir = prior_of(right_pack[0].astype(jnp.int32), right_pack[1])

    def squares(residual):
        return rows_sum(jnp.sum(residual * residual, axis=0))

    residual = prior_of(class_label, confidence)
    direction = residual
    left_res, right_res = left_dir, right_dir
    solution = jnp.zeros_like(residual)
    norm_now = None
    for step in range(ITERS):
        product_sum = block_product(
            graph_tiles,
            local_col,
            tile_count,
            left_dir.astype(jnp.bfloat16),
            direction.astype(jnp.bfloat16),
            right_dir.astype(jnp.bfloat16),
        )
        applied = direction - damping * product_sum
        left_app, right_app = halos(applied, ROWS, halo_rows, 0)
        curve_part = jnp.sum(direction * applied, axis=0)
        if step < ITERS - 1:
            curve_part = curve_part + 0.0 * (left_app[0] + right_app[0])
        if norm_now is None:
            both = rows_sum(jnp.stack([jnp.sum(residual * residual, axis=0), curve_part]))
            norm_now, curve_sum = both[0], both[1]
        else:
            curve_sum = rows_sum(curve_part)
        step_size = norm_now / curve_sum
        solution = solution + step_size[None, :] * direction
        residual = residual - step_size[None, :] * applied
        left_res = left_res - step_size[None, :] * left_app
        right_res = right_res - step_size[None, :] * right_app
        norm_next = squares(residual)
        ratio = (norm_next / norm_now)[None, :]
        direction = residual + ratio * direction
        left_dir = left_res + ratio * left_dir
        right_dir = right_res + ratio * right_dir
        norm_now = norm_next
    row_squares = cols_sum(jnp.sum(solution * solution, axis=1))
    length = jnp.sqrt(row_squares + 1e-06)
    return (solution / length[:, None], residual)


def factor(devices, pick):
    total = devices.shape[0]
    inner = len({pick(d) for d in devices})
    if inner < 1 or total % inner:
        return (1, total)
    return (total // inner, inner)


def solution(mesh):
    grid = mesh.devices
    row_shape = factor(grid[:, 0], lambda d: d.coords[2])
    col_shape = factor(grid[0, :], lambda d: d.core_on_chip)
    split = Mesh(grid.reshape(row_shape + col_shape), ROWS + COLS)
    placed = (
        P(ROWS, None, None, None),
        P(ROWS, None),
        P(ROWS),
        P(ROWS),
        P(ROWS),
        P(COLS),
    )
    return jax.shard_map(
        body,
        mesh=split,
        in_specs=placed,
        out_specs=(P(ROWS, COLS), P(ROWS, COLS)),
        check_vma=False,
    )
```

```python
import jax
import jax.numpy as jnp
from jax import lax
from jax.experimental import pallas as pl
from jax.experimental.pallas import tpu as pltpu
from jax.sharding import Mesh, PartitionSpec as P

ITERS = 3
ROWS = ("rx", "rz")
COLS = ("cy", "cc")


damping = 0.99
smoothing = 0.1


def padded(cells, sides, width):
    for axis, dim in sides:
        count = lax.axis_size(axis)
        head = lax.slice_in_dim(cells, 0, width, axis=dim)
        tail = lax.slice_in_dim(cells, cells.shape[dim] - width, cells.shape[dim], axis=dim)
        cells = jnp.concatenate(
            [
                lax.ppermute(tail, axis, [(i, (i + 1) % count) for i in range(count)]),
                cells,
                lax.ppermute(head, axis, [((i + 1) % count, i) for i in range(count)]),
            ],
            axis=dim,
        )
    return cells


def rows_sum(v):
    count = lax.axis_size(ROWS)
    spread = jnp.broadcast_to(v[None], (count,) + v.shape)
    gathered = lax.all_to_all(spread, ROWS, 0, 0, tiled=True)
    return jnp.sum(gathered, axis=0)


def cols_sum(v):
    count = lax.axis_size(COLS)
    spread = jnp.broadcast_to(v[None], (count,) + v.shape)
    gathered = lax.all_to_all(spread, COLS, 0, 0, tiled=True)
    return jnp.sum(gathered, axis=0)


def tile_kernel(
    col_ref, count_ref, tile_ref, left_ref, mid_ref, right_ref, dir_ref, out_ref, part_ref, vec_ref
):
    step = pl.program_id(0)
    group, slots, size, _ = tile_ref.shape
    head = left_ref.shape[0]
    middle = mid_ref.shape[0]

    @pl.when(step == 0)
    def _():
        vec_ref[pl.ds(0, head), :] = left_ref[...]
        vec_ref[pl.ds(head, middle), :] = mid_ref[...]
        vec_ref[pl.ds(head + middle, right_ref.shape[0]), :] = right_ref[...]

    total = jnp.zeros(part_ref.shape[1:], jnp.float32)
    for inner in range(group):
        row = step * group + inner
        live = count_ref[row]
        lhs = jnp.concatenate([tile_ref[inner, slot] for slot in range(slots)], axis=1)
        pieces = []
        for slot in range(slots):
            start = pl.multiple_of(col_ref[row * slots + slot] * size, size)
            block = vec_ref[pl.ds(start, size), :]
            pieces.append(jnp.where(slot < live, block, jnp.zeros_like(block)))
        rhs = jnp.concatenate(pieces, axis=0)
        product = jnp.dot(lhs, rhs, preferred_element_type=jnp.float32)
        direction = dir_ref[pl.ds(inner * size, size), :]
        applied = direction - damping * product
        out_ref[pl.ds(inner * size, size), :] = applied
        total = total + jnp.sum(direction * applied, axis=0, keepdims=True)
    part_ref[0] = total


def block_product(graph_tiles, local_col, tile_count, left, middle, right, direction):
    block_rows, slot_count, size, _ = graph_tiles.shape
    width = middle.shape[1]
    total = left.shape[0] + middle.shape[0] + right.shape[0]
    group = max(g for g in (1, 2, 4, 8) if block_rows % g == 0)
    whole = lambda r, c, n: (0, 0)
    grid_spec = pltpu.PrefetchScalarGridSpec(
        num_scalar_prefetch=2,
        grid=(block_rows // group,),
        in_specs=[
            pl.BlockSpec((group, slot_count, size, size), lambda r, c, n: (r, 0, 0, 0)),
            pl.BlockSpec(left.shape, whole),
            pl.BlockSpec(middle.shape, whole),
            pl.BlockSpec(right.shape, whole),
            pl.BlockSpec((group * size, width), lambda r, c, n: (r, 0)),
        ],
        out_specs=[
            pl.BlockSpec((group * size, width), lambda r, c, n: (r, 0)),
            pl.BlockSpec((1, 1, width), lambda r, c, n: (r, 0, 0)),
        ],
        scratch_shapes=[pltpu.VMEM((total, width), middle.dtype)],
    )
    cost = pl.CostEstimate(
        flops=2 * block_rows * slot_count * size * size * width,
        bytes_accessed=graph_tiles.size * 2 + total * width * 2 + block_rows * size * width * 8,
        transcendentals=0,
    )
    return pl.pallas_call(
        tile_kernel,
        grid_spec=grid_spec,
        out_shape=[
            jax.ShapeDtypeStruct((block_rows * size, width), jnp.float32),
            jax.ShapeDtypeStruct((block_rows // group, 1, width), jnp.float32),
        ],
        cost_estimate=cost,
    )(local_col.reshape(-1), tile_count, graph_tiles, left, middle, right, direction)


def halos(cells, axis, width, dim):
    count = lax.axis_size(axis)
    head = lax.slice_in_dim(cells, 0, width, axis=dim)
    tail = lax.slice_in_dim(cells, cells.shape[dim] - width, cells.shape[dim], axis=dim)
    left = lax.ppermute(tail, axis, [(i, (i + 1) % count) for i in range(count)])
    right = lax.ppermute(head, axis, [((i + 1) % count, i) for i in range(count)])
    return left, right


def body(graph_tiles, tile_column, tile_count, class_label, confidence, class_weight):
    block_rows = graph_tiles.shape[0]
    slot_count = graph_tiles.shape[1]
    block_size = graph_tiles.shape[2]
    class_dev = class_weight.shape[0]
    half_span = block_rows // 2
    total_blocks = block_rows * lax.axis_size(ROWS)
    first_row = lax.axis_index(ROWS) * block_rows - half_span
    live_slot = jnp.arange(slot_count, dtype=jnp.int32)[None, :] < tile_count[:, None]
    local_col = jnp.where(live_slot, jnp.mod(tile_column - first_row, total_blocks), 0)
    class_ids = lax.axis_index(COLS) * class_dev + jnp.arange(class_dev, dtype=jnp.int32)
    halo_rows = half_span * block_size
    spread = smoothing / (class_dev * lax.axis_size(COLS))

    def prior_of(label, weight):
        onehot = (label[:, None] == class_ids[None, :]).astype(jnp.float32)
        return weight[:, None] * class_weight[None, :] * ((1.0 - smoothing) * onehot + spread)

    packed = jnp.stack([class_label.astype(jnp.float32), confidence])
    left_pack, right_pack = halos(packed, ROWS, halo_rows, 1)
    left_dir = prior_of(left_pack[0].astype(jnp.int32), left_pack[1])
    right_dir = prior_of(right_pack[0].astype(jnp.int32), right_pack[1])

    def squares(residual):
        return rows_sum(jnp.sum(residual * residual, axis=0))

    residual = prior_of(class_label, confidence)
    direction = residual
    left_res, right_res = left_dir, right_dir
    solution = jnp.zeros_like(residual)
    norm_now = None
    for step in range(ITERS):
        product_sum = block_product(
            graph_tiles,
            local_col,
            tile_count,
            left_dir.astype(jnp.bfloat16),
            direction.astype(jnp.bfloat16),
            right_dir.astype(jnp.bfloat16),
            direction,
        )
        applied, parts = product_sum
        left_app, right_app = halos(applied, ROWS, halo_rows, 0)
        curve_part = jnp.sum(parts, axis=(0, 1))
        if norm_now is None:
            both = rows_sum(jnp.stack([jnp.sum(residual * residual, axis=0), curve_part]))
            norm_now, curve_sum = both[0], both[1]
        else:
            curve_sum = rows_sum(curve_part)
        step_size = norm_now / curve_sum
        solution = solution + step_size[None, :] * direction
        residual = residual - step_size[None, :] * applied
        left_res = left_res - step_size[None, :] * left_app
        right_res = right_res - step_size[None, :] * right_app
        norm_next = squares(residual)
        ratio = (norm_next / norm_now)[None, :]
        direction = residual + ratio * direction
        left_dir = left_res + ratio * left_dir
        right_dir = right_res + ratio * right_dir
        norm_now = norm_next
    row_squares = cols_sum(jnp.sum(solution * solution, axis=1))
    length = jnp.sqrt(row_squares + 1e-06)
    return (solution / length[:, None], residual)


def factor(devices, pick):
    total = devices.shape[0]
    inner = len({pick(d) for d in devices})
    if inner < 1 or total % inner:
        return (1, total)
    return (total // inner, inner)


def solution(mesh):
    grid = mesh.devices
    row_shape = factor(grid[:, 0], lambda d: d.coords[2])
    col_shape = factor(grid[0, :], lambda d: d.core_on_chip)
    split = Mesh(grid.reshape(row_shape + col_shape), ROWS + COLS)
    placed = (
        P(ROWS, None, None, None),
        P(ROWS, None),
        P(ROWS),
        P(ROWS),
        P(ROWS),
        P(COLS),
    )
    return jax.shard_map(
        body,
        mesh=split,
        in_specs=placed,
        out_specs=(P(ROWS, COLS), P(ROWS, COLS)),
        check_vma=False,
    )
```

```python
import jax
import jax.numpy as jnp
from jax import lax
from jax.experimental import pallas as pl
from jax.experimental.pallas import tpu as pltpu
from jax.sharding import Mesh, PartitionSpec as P

ITERS = 3
ROWS = ("rx", "rz")
COLS = ("cy", "cc")


damping = 0.99
smoothing = 0.1


def padded(cells, sides, width):
    for axis, dim in sides:
        count = lax.axis_size(axis)
        head = lax.slice_in_dim(cells, 0, width, axis=dim)
        tail = lax.slice_in_dim(cells, cells.shape[dim] - width, cells.shape[dim], axis=dim)
        cells = jnp.concatenate(
            [
                lax.ppermute(tail, axis, [(i, (i + 1) % count) for i in range(count)]),
                cells,
                lax.ppermute(head, axis, [((i + 1) % count, i) for i in range(count)]),
            ],
            axis=dim,
        )
    return cells


def rows_sum(v):
    count = lax.axis_size(ROWS)
    spread = jnp.broadcast_to(v[None], (count,) + v.shape)
    gathered = lax.all_to_all(spread, ROWS, 0, 0, tiled=True)
    return jnp.sum(gathered, axis=0)


def cols_sum(v):
    count = lax.axis_size(COLS)
    spread = jnp.broadcast_to(v[None], (count,) + v.shape)
    gathered = lax.all_to_all(spread, COLS, 0, 0, tiled=True)
    return jnp.sum(gathered, axis=0)


def local_kernel(col_ref, live_ref, tile_ref, mid_ref, out_ref):
    step = pl.program_id(0)
    group, slots, size, _ = tile_ref.shape
    for inner in range(group):
        row = step * group + inner
        lhs = jnp.concatenate([tile_ref[inner, slot] for slot in range(slots)], axis=1)
        pieces = []
        for slot in range(slots):
            start = pl.multiple_of(col_ref[row * slots + slot] * size, size)
            block = mid_ref[pl.ds(start, size), :]
            keep = live_ref[row * slots + slot] > 0
            pieces.append(jnp.where(keep, block, jnp.zeros_like(block)))
        rhs = jnp.concatenate(pieces, axis=0)
        out_ref[pl.ds(inner * size, size), :] = jnp.dot(
            lhs, rhs, preferred_element_type=jnp.float32
        )


def halo_kernel(slot_ref, live_ref, col_ref, tile_ref, left_ref, right_ref, part_ref, out_ref, vec_ref):
    step = pl.program_id(0)
    group, _, size, _ = tile_ref.shape
    head = left_ref.shape[0]
    picks = slot_ref.shape[0] // (group * pl.num_programs(0))

    @pl.when(step == 0)
    def _():
        vec_ref[pl.ds(0, head), :] = left_ref[...]
        vec_ref[pl.ds(head, right_ref.shape[0]), :] = right_ref[...]

    for inner in range(group):
        row = step * group + inner
        lhs_parts = []
        pieces = []
        for pick in range(picks):
            at = row * picks + pick
            lhs_parts.append(tile_ref[inner, slot_ref[at]])
            start = pl.multiple_of(col_ref[at] * size, size)
            block = vec_ref[pl.ds(start, size), :]
            pieces.append(jnp.where(live_ref[at] > 0, block, jnp.zeros_like(block)))
        lhs = jnp.concatenate(lhs_parts, axis=1)
        rhs = jnp.concatenate(pieces, axis=0)
        rows = pl.ds(inner * size, size)
        out_ref[rows, :] = part_ref[rows, :] + jnp.dot(
            lhs, rhs, preferred_element_type=jnp.float32
        )


def row_group(block_rows):
    return max(g for g in (1, 2, 4, 8) if block_rows % g == 0)


def local_product(graph_tiles, local_slot, local_live, middle):
    block_rows, slot_count, size, _ = graph_tiles.shape
    width = middle.shape[1]
    group = row_group(block_rows)
    grid_spec = pltpu.PrefetchScalarGridSpec(
        num_scalar_prefetch=2,
        grid=(block_rows // group,),
        in_specs=[
            pl.BlockSpec((group, slot_count, size, size), lambda r, c, n: (r, 0, 0, 0)),
            pl.BlockSpec(middle.shape, lambda r, c, n: (0, 0)),
        ],
        out_specs=pl.BlockSpec((group * size, width), lambda r, c, n: (r, 0)),
    )
    cost = pl.CostEstimate(
        flops=2 * block_rows * slot_count * size * size * width,
        bytes_accessed=graph_tiles.size * 2 + middle.size * 2 + block_rows * size * width * 4,
        transcendentals=0,
    )
    return pl.pallas_call(
        local_kernel,
        grid_spec=grid_spec,
        out_shape=jax.ShapeDtypeStruct((block_rows * size, width), jnp.float32),
        cost_estimate=cost,
    )(local_slot.reshape(-1), local_live.reshape(-1), graph_tiles, middle)


def halo_product(graph_tiles, halo_slot, halo_live, halo_col, left, right, part):
    block_rows, slot_count, size, _ = graph_tiles.shape
    width = part.shape[1]
    picks = halo_slot.shape[1]
    group = row_group(block_rows)
    whole = lambda r, s, l, c: (0, 0)
    grid_spec = pltpu.PrefetchScalarGridSpec(
        num_scalar_prefetch=3,
        grid=(block_rows // group,),
        in_specs=[
            pl.BlockSpec((group, slot_count, size, size), lambda r, s, l, c: (r, 0, 0, 0)),
            pl.BlockSpec(left.shape, whole),
            pl.BlockSpec(right.shape, whole),
            pl.BlockSpec((group * size, width), lambda r, s, l, c: (r, 0)),
        ],
        out_specs=pl.BlockSpec((group * size, width), lambda r, s, l, c: (r, 0)),
        scratch_shapes=[pltpu.VMEM((left.shape[0] + right.shape[0], width), left.dtype)],
    )
    cost = pl.CostEstimate(
        flops=2 * block_rows * picks * size * size * width,
        bytes_accessed=graph_tiles.size * 2 + (left.size + right.size) * 2 + part.size * 8,
        transcendentals=0,
    )
    return pl.pallas_call(
        halo_kernel,
        grid_spec=grid_spec,
        out_shape=jax.ShapeDtypeStruct((block_rows * size, width), jnp.float32),
        cost_estimate=cost,
    )(halo_slot.reshape(-1), halo_live.reshape(-1), halo_col.reshape(-1), graph_tiles, left, right, part)


def halos(cells, axis, width, dim):
    count = lax.axis_size(axis)
    head = lax.slice_in_dim(cells, 0, width, axis=dim)
    tail = lax.slice_in_dim(cells, cells.shape[dim] - width, cells.shape[dim], axis=dim)
    left = lax.ppermute(tail, axis, [(i, (i + 1) % count) for i in range(count)])
    right = lax.ppermute(head, axis, [((i + 1) % count, i) for i in range(count)])
    return left, right


def body(graph_tiles, tile_column, tile_count, class_label, confidence, class_weight):
    block_rows = graph_tiles.shape[0]
    slot_count = graph_tiles.shape[1]
    block_size = graph_tiles.shape[2]
    class_dev = class_weight.shape[0]
    half_span = block_rows // 2
    total_blocks = block_rows * lax.axis_size(ROWS)
    first_row = lax.axis_index(ROWS) * block_rows - half_span
    live_slot = jnp.arange(slot_count, dtype=jnp.int32)[None, :] < tile_count[:, None]
    local_col = jnp.where(live_slot, jnp.mod(tile_column - first_row, total_blocks), 0)
    own_block = (local_col >= half_span) & (local_col < half_span + block_rows)
    is_local = live_slot & own_block
    is_halo = live_slot & ~own_block
    local_slot = jnp.where(is_local, local_col - half_span, 0)
    order = jnp.argsort((~is_halo).astype(jnp.int32), axis=1, stable=True)[:, :half_span]
    halo_live = jnp.take_along_axis(is_halo, order, axis=1)
    halo_ext = jnp.take_along_axis(local_col, order, axis=1)
    halo_col = jnp.where(
        halo_live, jnp.where(halo_ext < half_span, halo_ext, halo_ext - block_rows), 0
    )
    class_ids = lax.axis_index(COLS) * class_dev + jnp.arange(class_dev, dtype=jnp.int32)
    halo_rows = half_span * block_size
    spread = smoothing / (class_dev * lax.axis_size(COLS))

    def prior_of(label, weight):
        onehot = (label[:, None] == class_ids[None, :]).astype(jnp.float32)
        return weight[:, None] * class_weight[None, :] * ((1.0 - smoothing) * onehot + spread)

    packed = jnp.stack([class_label.astype(jnp.float32), confidence])
    left_pack, right_pack = halos(packed, ROWS, halo_rows, 1)
    left_dir = prior_of(left_pack[0].astype(jnp.int32), left_pack[1])
    right_dir = prior_of(right_pack[0].astype(jnp.int32), right_pack[1])

    def squares(residual):
        return rows_sum(jnp.sum(residual * residual, axis=0))

    residual = prior_of(class_label, confidence)
    direction = residual
    left_res, right_res = left_dir, right_dir
    solution = jnp.zeros_like(residual)
    norm_now = None
    for step in range(ITERS):
        part = local_product(graph_tiles, local_slot, is_local.astype(jnp.int32), direction.astype(jnp.bfloat16))
        product_sum = halo_product(
            graph_tiles,
            order.astype(jnp.int32),
            halo_live.astype(jnp.int32),
            halo_col,
            left_dir.astype(jnp.bfloat16),
            right_dir.astype(jnp.bfloat16),
            part,
        )
        applied = direction - damping * product_sum
        left_app, right_app = halos(applied, ROWS, halo_rows, 0)
        curve_part = jnp.sum(direction * applied, axis=0)
        if norm_now is None:
            both = rows_sum(jnp.stack([jnp.sum(residual * residual, axis=0), curve_part]))
            norm_now, curve_sum = both[0], both[1]
        else:
            curve_sum = rows_sum(curve_part)
        step_size = norm_now / curve_sum
        solution = solution + step_size[None, :] * direction
        residual = residual - step_size[None, :] * applied
        left_res = left_res - step_size[None, :] * left_app
        right_res = right_res - step_size[None, :] * right_app
        norm_next = squares(residual)
        ratio = (norm_next / norm_now)[None, :]
        direction = residual + ratio * direction
        left_dir = left_res + ratio * left_dir
        right_dir = right_res + ratio * right_dir
        norm_now = norm_next
    row_squares = cols_sum(jnp.sum(solution * solution, axis=1))
    length = jnp.sqrt(row_squares + 1e-06)
    return (solution / length[:, None], residual)


def factor(devices, pick):
    total = devices.shape[0]
    inner = len({pick(d) for d in devices})
    if inner < 1 or total % inner:
        return (1, total)
    return (total // inner, inner)


def solution(mesh):
    grid = mesh.devices
    row_shape = factor(grid[:, 0], lambda d: d.coords[2])
    col_shape = factor(grid[0, :], lambda d: d.core_on_chip)
    split = Mesh(grid.reshape(row_shape + col_shape), ROWS + COLS)
    placed = (
        P(ROWS, None, None, None),
        P(ROWS, None),
        P(ROWS),
        P(ROWS),
        P(ROWS),
        P(COLS),
    )
    return jax.shard_map(
        body,
        mesh=split,
        in_specs=placed,
        out_specs=(P(ROWS, COLS), P(ROWS, COLS)),
        check_vma=False,
    )
```

```python
import jax
import jax.numpy as jnp
from jax import lax
from jax.experimental import pallas as pl
from jax.experimental.pallas import tpu as pltpu
from jax.sharding import Mesh, PartitionSpec as P

ITERS = 3
ROWS = ("rx", "rz")
COLS = ("cy", "cc")


damping = 0.99
smoothing = 0.1


def padded(cells, sides, width):
    for axis, dim in sides:
        count = lax.axis_size(axis)
        head = lax.slice_in_dim(cells, 0, width, axis=dim)
        tail = lax.slice_in_dim(cells, cells.shape[dim] - width, cells.shape[dim], axis=dim)
        cells = jnp.concatenate(
            [
                lax.ppermute(tail, axis, [(i, (i + 1) % count) for i in range(count)]),
                cells,
                lax.ppermute(head, axis, [((i + 1) % count, i) for i in range(count)]),
            ],
            axis=dim,
        )
    return cells


def rows_sum(v):
    count = lax.axis_size(ROWS)
    spread = jnp.broadcast_to(v[None], (count,) + v.shape)
    gathered = lax.all_to_all(spread, ROWS, 0, 0, tiled=True)
    return jnp.sum(gathered, axis=0)


def cols_sum(v):
    count = lax.axis_size(COLS)
    spread = jnp.broadcast_to(v[None], (count,) + v.shape)
    gathered = lax.all_to_all(spread, COLS, 0, 0, tiled=True)
    return jnp.sum(gathered, axis=0)


def tile_kernel(col_ref, count_ref, tile_ref, left_ref, mid_ref, right_ref, out_ref, vec_ref):
    step = pl.program_id(0)
    group, slots, size, _ = tile_ref.shape
    head = left_ref.shape[0]
    middle = mid_ref.shape[0]

    @pl.when(step == 0)
    def _():
        vec_ref[pl.ds(0, head), :] = left_ref[...]
        vec_ref[pl.ds(head, middle), :] = mid_ref[...]
        vec_ref[pl.ds(head + middle, right_ref.shape[0]), :] = right_ref[...]

    for inner in range(group):
        row = step * group + inner
        live = count_ref[row]
        lhs = jnp.concatenate([tile_ref[inner, slot] for slot in range(slots)], axis=1)
        pieces = []
        for slot in range(slots):
            start = pl.multiple_of(col_ref[row * slots + slot] * size, size)
            block = vec_ref[pl.ds(start, size), :]
            pieces.append(jnp.where(slot < live, block, jnp.zeros_like(block)))
        rhs = jnp.concatenate(pieces, axis=0)
        out_ref[pl.ds(inner * size, size), :] = jnp.dot(
            lhs, rhs, preferred_element_type=jnp.float32
        )


def block_product(graph_tiles, local_col, tile_count, left, middle, right):
    block_rows, slot_count, size, _ = graph_tiles.shape
    width = middle.shape[1]
    total = left.shape[0] + middle.shape[0] + right.shape[0]
    group = max(g for g in (1, 2, 4, 8) if block_rows % g == 0)
    whole = lambda r, c, n: (0, 0)
    grid_spec = pltpu.PrefetchScalarGridSpec(
        num_scalar_prefetch=2,
        grid=(block_rows // group,),
        in_specs=[
            pl.BlockSpec((group, slot_count, size, size), lambda r, c, n: (r, 0, 0, 0)),
            pl.BlockSpec(left.shape, whole),
            pl.BlockSpec(middle.shape, whole),
            pl.BlockSpec(right.shape, whole),
        ],
        out_specs=pl.BlockSpec((group * size, width), lambda r, c, n: (r, 0)),
        scratch_shapes=[pltpu.VMEM((total, width), middle.dtype)],
    )
    cost = pl.CostEstimate(
        flops=2 * block_rows * slot_count * size * size * width,
        bytes_accessed=graph_tiles.size * 2 + total * width * 2 + block_rows * size * width * 4,
        transcendentals=0,
    )
    return pl.pallas_call(
        tile_kernel,
        grid_spec=grid_spec,
        out_shape=jax.ShapeDtypeStruct((block_rows * size, width), jnp.float32),
        cost_estimate=cost,
    )(local_col.reshape(-1), tile_count, graph_tiles, left, middle, right)


def halos(cells, axis, width, dim):
    count = lax.axis_size(axis)
    head = lax.slice_in_dim(cells, 0, width, axis=dim)
    tail = lax.slice_in_dim(cells, cells.shape[dim] - width, cells.shape[dim], axis=dim)
    left = lax.ppermute(tail, axis, [(i, (i + 1) % count) for i in range(count)])
    right = lax.ppermute(head, axis, [((i + 1) % count, i) for i in range(count)])
    return left, right


def body(graph_tiles, tile_column, tile_count, class_label, confidence, class_weight):
    block_rows = graph_tiles.shape[0]
    slot_count = graph_tiles.shape[1]
    block_size = graph_tiles.shape[2]
    class_dev = class_weight.shape[0]
    half_span = block_rows // 2
    total_blocks = block_rows * lax.axis_size(ROWS)
    first_row = lax.axis_index(ROWS) * block_rows - half_span
    live_slot = jnp.arange(slot_count, dtype=jnp.int32)[None, :] < tile_count[:, None]
    local_col = jnp.where(live_slot, jnp.mod(tile_column - first_row, total_blocks), 0)
    class_ids = lax.axis_index(COLS) * class_dev + jnp.arange(class_dev, dtype=jnp.int32)
    halo_rows = half_span * block_size
    spread = smoothing / (class_dev * lax.axis_size(COLS))

    def prior_of(label, weight):
        onehot = (label[:, None] == class_ids[None, :]).astype(jnp.float32)
        return weight[:, None] * class_weight[None, :] * ((1.0 - smoothing) * onehot + spread)

    residual = prior_of(class_label, confidence)
    first_cast = residual.astype(jnp.bfloat16)
    anchor = 0.0 * (first_cast[0, 0].astype(jnp.float32) + local_col[0, 0].astype(jnp.float32))
    packed = jnp.stack([class_label.astype(jnp.float32), confidence + anchor])
    left_pack, right_pack = halos(packed, ROWS, halo_rows, 1)
    left_dir = prior_of(left_pack[0].astype(jnp.int32), left_pack[1])
    right_dir = prior_of(right_pack[0].astype(jnp.int32), right_pack[1])

    def squares(residual):
        return rows_sum(jnp.sum(residual * residual, axis=0))

    direction = residual
    left_res, right_res = left_dir, right_dir
    solution = jnp.zeros_like(residual)
    norm_now = None
    for step in range(ITERS):
        product_sum = block_product(
            graph_tiles,
            local_col,
            tile_count,
            left_dir.astype(jnp.bfloat16),
            direction.astype(jnp.bfloat16),
            right_dir.astype(jnp.bfloat16),
        )
        applied = direction - damping * product_sum
        left_app, right_app = halos(applied, ROWS, halo_rows, 0)
        curve_part = jnp.sum(direction * applied, axis=0)
        if norm_now is None:
            both = rows_sum(jnp.stack([jnp.sum(residual * residual, axis=0), curve_part]))
            norm_now, curve_sum = both[0], both[1]
        else:
            curve_sum = rows_sum(curve_part)
        step_size = norm_now / curve_sum
        solution = solution + step_size[None, :] * direction
        residual = residual - step_size[None, :] * applied
        left_res = left_res - step_size[None, :] * left_app
        right_res = right_res - step_size[None, :] * right_app
        norm_next = squares(residual)
        ratio = (norm_next / norm_now)[None, :]
        direction = residual + ratio * direction
        left_dir = left_res + ratio * left_dir
        right_dir = right_res + ratio * right_dir
        norm_now = norm_next
    row_squares = cols_sum(jnp.sum(solution * solution, axis=1))
    length = jnp.sqrt(row_squares + 1e-06)
    return (solution / length[:, None], residual)


def factor(devices, pick):
    total = devices.shape[0]
    inner = len({pick(d) for d in devices})
    if inner < 1 or total % inner:
        return (1, total)
    return (total // inner, inner)


def solution(mesh):
    grid = mesh.devices
    row_shape = factor(grid[:, 0], lambda d: d.coords[2])
    col_shape = factor(grid[0, :], lambda d: d.core_on_chip)
    split = Mesh(grid.reshape(row_shape + col_shape), ROWS + COLS)
    placed = (
        P(ROWS, None, None, None),
        P(ROWS, None),
        P(ROWS),
        P(ROWS),
        P(ROWS),
        P(COLS),
    )
    return jax.shard_map(
        body,
        mesh=split,
        in_specs=placed,
        out_specs=(P(ROWS, COLS), P(ROWS, COLS)),
        check_vma=False,
    )
```
